32 devices in a mesh: ta: 4 (over z), xyz: 8 (over y, x, core).
Axes of the slice: x: 2, y: 2, z: 4, core: 2. Of those that a mesh axis runs over, the one named last changes fastest.
Arguments:
- right_side: float32 [32, 4, 8, 4, 2, 2, 128], P(None, 'ta', 'xyz'), may hold values from -6 to 6
- coarse_links: bfloat16 [4, 8, 4, 2, 2, 9, 64, 128], P('ta', 'xyz'), may hold values from -3 to 3
- null_vectors: bfloat16 [4, 8, 4, 2, 2, 48, 128], P('ta', 'xyz'), may hold values from -0.29882812 to 0.29882812
- coarse_inverse: bfloat16 [4, 384, 384], P('ta', 'xyz'), may hold values from -2 to 2
Outputs:
- solution: float32 [32, 4, 8, 4, 2, 2, 128], P(None, 'ta', 'xyz')
- residual: float32 [32, 4, 8, 4, 2, 2, 128], P(None, 'ta', 'xyz')
The draws below stay inside these ranges and needn't reach their ends.
All inputs are finite; a program needn't handle non-finite values.
Results may differ from the reference program's by a relative error of at most 0.0075.
Values may be sent and summed in bfloat16 or wider, within the bound.
No kernel may reach another device: no remote copies, remote signals or barrier semaphores. Data moves between devices by JAX's collectives and lax.ppermute only.
A program may use at most 64 MiB of HBM per device.

```python
import math
import jax
import jax.numpy as jnp
from jax import lax

NC = 64
NRHS = 32
LZ = 4
LY = 2
LX = 2
BX = 2
BZ = 2
CV = 48
NT = 4
NZ = 8
NY = 4
NX = 4
GROUP_CV = 384
N_TA = 4
N_XYZ = 8


def draw_coarse_links(key, part):
    shape = (NT, N_XYZ, LZ, LY, LX, 9, NC, 2 * NC)
    noise = jnp.clip(jax.random.normal(key, shape, jnp.float32), -4.0, 4.0)
    small = (9, NC, 2 * NC)
    block = lax.broadcasted_iota(jnp.int32, small, 0)
    row_index = lax.broadcasted_iota(jnp.int32, small, 1)
    col_index = lax.broadcasted_iota(jnp.int32, small, 2)
    diagonal = jnp.where((block == 0) & (row_index == col_index), 2.0, 0.0).astype(jnp.float32)
    spread = jnp.where(block == 0, 0.6, 0.35).astype(jnp.float32) / math.sqrt(2 * NC)
    return (diagonal + spread * noise).astype(jnp.bfloat16)


def draw_coarse_inverse(key, part):
    shape = (N_TA, GROUP_CV, GROUP_CV)
    noise = jnp.clip(jax.random.normal(key, shape, jnp.float32), -4.0, 4.0)
    row_index = lax.broadcasted_iota(jnp.int32, shape, 1)
    col_index = lax.broadcasted_iota(jnp.int32, shape, 2)
    diagonal = jnp.where(row_index == col_index, 1.0, 0.0).astype(jnp.float32)
    return (diagonal + noise / math.sqrt(GROUP_CV)).astype(jnp.bfloat16)


def steps_of(stream_key, shape, split, least, largest):
    def one(position, shards_of):
        steps = jax.random.uniform(jax.random.fold_in(jax.random.fold_in(stream_key, 6), position), (shards_of,), jnp.float32, least / len(split), largest / len(split))
        return jnp.repeat(jnp.exp(steps), shape[position] // shards_of).reshape((-1,) + (1,) * (len(shape) - position - 1))

    level = one(*split[0])
    for cut in split[1:]:
        level = level * one(*cut)
    return level


def scatter_about(stream_key, extent, scale, bound, split=(), dtype=jnp.bfloat16):
    entries = scale * jax.random.normal(stream_key, extent, jnp.float32)
    if split:
        entries = entries * steps_of(stream_key, extent, split, -0.22, 0.18)
    return jnp.clip(entries, -bound, bound).astype(dtype)


def setup_inputs(seed: int = 0) -> dict:
    key_list = jax.random.split(jax.random.key(seed), 5)
    right_side = scatter_about(key_list[0], (NRHS, NT, N_XYZ, LZ, LY, LX, 2 * NC), 1.0, 6.0, ((1, 4), (2, 8)), jnp.float32)
    coarse_links = draw_coarse_links(jax.random.fold_in(key_list[4], 71), 0)
    null_vectors = scatter_about(key_list[2], (NT, N_XYZ, LZ, LY, LX, CV, 2 * NC), 0.05, 0.29882812, ((0, 4), (1, 8)))
    coarse_inverse = draw_coarse_inverse(jax.random.fold_in(key_list[4], 71), 0)
    return {"right_side": right_side, "coarse_links": coarse_links, "null_vectors": null_vectors, "coarse_inverse": coarse_inverse}


OMEGA = 0.4
EPS = 1e-6
MOVES = [(4, -1), (4, 1), (3, -1), (3, 1), (2, -1), (2, 1), (1, -1), (1, 1)]


def to_lattice(field):
    count = field.shape[0]
    width = field.shape[-1]
    blocks = field.reshape(count, NT, BZ, BX, BX, LZ, LY, LX, width)
    blocks = jnp.transpose(blocks, (0, 1, 2, 5, 3, 6, 4, 7, 8))
    return blocks.reshape(count, NT, NZ, NY, NX, width)


def to_blocks(lattice):
    count = lattice.shape[0]
    width = lattice.shape[-1]
    blocks = lattice.reshape(count, NT, BZ, LZ, BX, LY, BX, LX, width)
    blocks = jnp.transpose(blocks, (0, 1, 2, 4, 6, 3, 5, 7, 8))
    return blocks.reshape(count, NT, N_XYZ, LZ, LY, LX, width)


def apply_links(coarse_links, lowered):
    lattice = to_lattice(lowered)
    shifted = [lowered] + [to_blocks(jnp.roll(lattice, amount, axis=which)) for which, amount in MOVES]
    stacked = jnp.stack(shifted, 1)
    half_width = lowered.shape[-1] // 2
    real_part = stacked[..., :half_width]
    imag_part = stacked[..., half_width:]
    real_input = jnp.concatenate([real_part, -imag_part], -1)
    imag_input = jnp.concatenate([imag_part, real_part], -1)
    inputs = jnp.moveaxis(jnp.stack([real_input, imag_input], 0), 3, 0)

    def one_slice(pair):
        return jnp.einsum("bzyxdik,pndbzyxk->pnbzyxi", pair[0].astype(jnp.float32), pair[1].astype(jnp.float32))

    result = jnp.moveaxis(lax.map(one_slice, (coarse_links, inputs)), 0, 2)
    return jnp.concatenate([result[0], result[1]], -1)


def precondition(vector_in, null_vectors, coarse_inverse):
    count = vector_in.shape[0]
    lowered = vector_in.astype(jnp.bfloat16)
    blocked = null_vectors.astype(jnp.float32)
    rows = lowered.astype(jnp.float32)
    coarse = jnp.einsum("tbzyxjk,ntbzyxk->ntbj", blocked, rows).astype(jnp.bfloat16)
    flat = coarse.reshape(count, NT, N_XYZ * CV).astype(jnp.float32)
    correction = jnp.einsum("trc,ntc->ntr", coarse_inverse.astype(jnp.float32), flat).astype(jnp.bfloat16)
    correction = correction.reshape(count, NT, N_XYZ, CV).astype(jnp.float32)
    prolonged = jnp.einsum("tbzyxjk,ntbj->ntbzyxk", blocked, correction)
    return OMEGA * vector_in + prolonged


def inner_rows(left_vec, right_vec):
    return jnp.sum(left_vec * right_vec, axis=(1, 2, 3, 4, 5, 6))


def scaled(weights, vector_in):
    return weights[:, None, None, None, None, None, None] * vector_in


def reference(right_side, coarse_links, null_vectors, coarse_inverse):
    residual = right_side
    direction_a = precondition(residual, null_vectors, coarse_inverse)
    image_a = apply_links(coarse_links, direction_a.astype(jnp.bfloat16))
    norm_a = inner_rows(image_a, image_a)
    step_a = inner_rows(image_a, residual) / (norm_a + EPS)
    solution = scaled(step_a, direction_a)
    residual = residual - scaled(step_a, image_a)
    direction_b = precondition(residual, null_vectors, coarse_inverse)
    image_b = apply_links(coarse_links, direction_b.astype(jnp.bfloat16))
    beta_coef = inner_rows(image_a, image_b) / (norm_a + EPS)
    image_b = image_b - scaled(beta_coef, image_a)
    direction_b = direction_b - scaled(beta_coef, direction_a)
    step_b = inner_rows(image_b, residual) / (inner_rows(image_b, image_b) + EPS)
    solution = solution + scaled(step_b, direction_b)
    residual = residual - scaled(step_b, image_b)
    return solution, residual
```

```python
import jax
import jax.numpy as jnp
from jax import lax
from jax.sharding import PartitionSpec as P

OMEGA = 0.4
EPS = 1e-06


def is_power_of_two(count):
    return count & (count - 1) == 0


def exchange(x, axis, bit):
    count = lax.axis_size(axis)
    return lax.ppermute(x, axis, [(i, i ^ bit) for i in range(count)])


def axis_sum(x, axis):
    count = lax.axis_size(axis)
    if not is_power_of_two(count):
        return lax.psum(x, axis)
    bit = 1
    while bit < count:
        x = x + exchange(x, axis, bit)
        bit *= 2
    return x


def total_sum(x):
    return axis_sum(axis_sum(x, "xyz"), "ta")


def gather_tiled(x, axis, dim):
    count = lax.axis_size(axis)
    if not is_power_of_two(count):
        return lax.all_gather(x, axis, axis=dim, tiled=True)
    me = lax.axis_index(axis)
    bit = 1
    while bit < count:
        other = exchange(x, axis, bit)
        x = jnp.where(
            me // bit % 2 == 0,
            jnp.concatenate([x, other], dim),
            jnp.concatenate([other, x], dim),
        )
        bit *= 2
    return x


def neighbour_source(device, stride, extent, step):
    coord = device // stride % extent
    return device + ((coord + step) % extent - coord) * stride


def both_sides(lowered, which, axis, stride, extent):
    length = lowered.shape[which]
    count = lax.axis_size(axis)
    first = lax.slice_in_dim(lowered, 0, 1, axis=which)
    last = lax.slice_in_dim(lowered, length - 1, length, axis=which)
    if extent == 1:
        from_upper, from_lower = first, last
    elif extent == 2:
        perm = [(neighbour_source(d, stride, extent, 1), d) for d in range(count)]
        if length == 1:
            from_upper = from_lower = lax.ppermute(first, axis, perm)
        else:
            pair = lax.ppermute(jnp.concatenate([first, last], which), axis, perm)
            from_upper = lax.slice_in_dim(pair, 0, 1, axis=which)
            from_lower = lax.slice_in_dim(pair, 1, 2, axis=which)
    else:
        up = [(neighbour_source(d, stride, extent, 1), d) for d in range(count)]
        down = [(neighbour_source(d, stride, extent, -1), d) for d in range(count)]
        from_upper = lax.ppermute(first, axis, up)
        from_lower = lax.ppermute(last, axis, down)
    upper = jnp.concatenate([lax.slice_in_dim(lowered, 1, length, axis=which), from_upper], which)
    lower = jnp.concatenate(
        [from_lower, lax.slice_in_dim(lowered, 0, length - 1, axis=which)], which
    )
    return (upper, lower)


def apply_links(coarse_links, lowered):
    blocks_total = lax.axis_size("xyz")
    across_x = 2 + 2 * min(blocks_total // 64, 1)
    across_z = blocks_total // (across_x * across_x)
    upper_x, lower_x = both_sides(lowered, 5, "xyz", 1, across_x)
    upper_y, lower_y = both_sides(lowered, 4, "xyz", across_x, across_x)
    upper_z, lower_z = both_sides(lowered, 3, "xyz", across_x * across_x, across_z)
    upper_t, lower_t = both_sides(lowered, 1, "ta", 1, lax.axis_size("ta"))
    stacked = jnp.stack(
        [lowered, upper_x, lower_x, upper_y, lower_y, upper_z, lower_z, upper_t, lower_t], 2
    )
    half_width = lowered.shape[-1] // 2
    real_part = stacked[..., :half_width]
    imag_part = stacked[..., half_width:]
    real_input = jnp.concatenate([real_part, -imag_part], -1)
    imag_input = jnp.concatenate([imag_part, real_part], -1)
    inputs = jnp.stack([real_input, imag_input], 0)
    result = jnp.einsum(
        "tbzyxdik,pntdbzyxk->pntbzyxi", coarse_links, inputs, preferred_element_type=jnp.float32
    )
    return jnp.concatenate([result[0], result[1]], -1)


def precondition(vector_in, null_vectors, coarse_inverse):
    lowered = vector_in.astype(jnp.bfloat16)
    coarse = jnp.einsum(
        "tbzyxjk,ntbzyxk->nj", null_vectors, lowered, preferred_element_type=jnp.float32
    ).astype(jnp.bfloat16)
    inverse_rows = coarse_inverse[0]
    correction = lax.dot_general(
        gather_tiled(coarse, "xyz", 1),
        inverse_rows,
        (((1,), (1,)), ((), ())),
        preferred_element_type=jnp.float32,
    ).astype(jnp.bfloat16)
    prolonged = jnp.einsum(
        "tbzyxjk,nj->ntbzyxk", null_vectors, correction, preferred_element_type=jnp.float32
    )
    return OMEGA * vector_in + prolonged


def inner_rows(left_vec, right_vec):
    return jnp.sum(left_vec * right_vec, axis=(1, 2, 3, 4, 5, 6))


def scaled(weights, vector_in):
    return weights[:, None, None, None, None, None, None] * vector_in


def pair_products(image, residual):
    both = total_sum(jnp.stack([inner_rows(image, image), inner_rows(image, residual)]))
    return (both[0], both[1])


def shards(right_side, coarse_links, null_vectors, coarse_inverse):
    residual = right_side
    direction_a = precondition(residual, null_vectors, coarse_inverse)
    image_a = apply_links(coarse_links, direction_a.astype(jnp.bfloat16))
    norm_a, correlation_a = pair_products(image_a, residual)
    step_a = correlation_a / (norm_a + EPS)
    solution = scaled(step_a, direction_a)
    residual = residual - scaled(step_a, image_a)
    direction_b = precondition(residual, null_vectors, coarse_inverse)
    image_b = apply_links(coarse_links, direction_b.astype(jnp.bfloat16))
    projection_sum = total_sum(inner_rows(image_a, image_b))
    beta_coef = projection_sum / (norm_a + EPS)
    image_b = image_b - scaled(beta_coef, image_a)
    direction_b = direction_b - scaled(beta_coef, direction_a)
    norm_b, correlation_b = pair_products(image_b, residual)
    step_b = correlation_b / (norm_b + EPS)
    solution = solution + scaled(step_b, direction_b)
    residual = residual - scaled(step_b, image_b)
    return (solution, residual)


def solution(mesh):
    in_specs = (
        P(None, "ta", "xyz", None, None, None, None),
        P("ta", "xyz", None, None, None, None, None, None),
        P("ta", "xyz", None, None, None, None, None),
        P("ta", "xyz", None),
    )
    out_specs = (
        P(None, "ta", "xyz", None, None, None, None),
        P(None, "ta", "xyz", None, None, None, None),
    )
    return jax.shard_map(shards, mesh=mesh, in_specs=in_specs, out_specs=out_specs, check_vma=False)
```

```python
import jax
import jax.numpy as jnp
from jax import lax
from jax.sharding import PartitionSpec as P

OMEGA = 0.4
EPS = 1e-06


def is_power_of_two(count):
    return count & (count - 1) == 0


def exchange(x, axis, bit):
    count = lax.axis_size(axis)
    return lax.ppermute(x, axis, [(i, i ^ bit) for i in range(count)])


def axis_sum(x, axis):
    count = lax.axis_size(axis)
    if not is_power_of_two(count):
        return lax.psum(x, axis)
    bit = 1
    while bit < count:
        x = x + exchange(x, axis, bit)
        bit *= 2
    return x


def total_sum(x):
    return axis_sum(axis_sum(x, "xyz"), "ta")


def gather_tiled(x, axis, dim):
    count = lax.axis_size(axis)
    if not is_power_of_two(count):
        return lax.all_gather(x, axis, axis=dim, tiled=True)
    me = lax.axis_index(axis)
    bit = 1
    while bit < count:
        other = exchange(x, axis, bit)
        x = jnp.where(
            me // bit % 2 == 0,
            jnp.concatenate([x, other], dim),
            jnp.concatenate([other, x], dim),
        )
        bit *= 2
    return x


def neighbour_source(device, stride, extent, step):
    coord = device // stride % extent
    return device + ((coord + step) % extent - coord) * stride


def both_sides(lowered, which, axis, stride, extent):
    length = lowered.shape[which]
    count = lax.axis_size(axis)
    first = lax.slice_in_dim(lowered, 0, 1, axis=which)
    last = lax.slice_in_dim(lowered, length - 1, length, axis=which)
    if extent == 1:
        from_upper, from_lower = first, last
    elif extent == 2:
        perm = [(neighbour_source(d, stride, extent, 1), d) for d in range(count)]
        if length == 1:
            from_upper = from_lower = lax.ppermute(first, axis, perm)
        else:
            pair = lax.ppermute(jnp.concatenate([first, last], which), axis, perm)
            from_upper = lax.slice_in_dim(pair, 0, 1, axis=which)
            from_lower = lax.slice_in_dim(pair, 1, 2, axis=which)
    else:
        up = [(neighbour_source(d, stride, extent, 1), d) for d in range(count)]
        down = [(neighbour_source(d, stride, extent, -1), d) for d in range(count)]
        from_upper = lax.ppermute(first, axis, up)
        from_lower = lax.ppermute(last, axis, down)
    upper = jnp.concatenate([lax.slice_in_dim(lowered, 1, length, axis=which), from_upper], which)
    lower = jnp.concatenate(
        [from_lower, lax.slice_in_dim(lowered, 0, length - 1, axis=which)], which
    )
    return (upper, lower)


def apply_links(coarse_links, lowered):
    blocks_total = lax.axis_size("xyz")
    across_x = 2 + 2 * min(blocks_total // 64, 1)
    across_z = blocks_total // (across_x * across_x)
    upper_x, lower_x = both_sides(lowered, 5, "xyz", 1, across_x)
    upper_y, lower_y = both_sides(lowered, 4, "xyz", across_x, across_x)
    upper_z, lower_z = both_sides(lowered, 3, "xyz", across_x * across_x, across_z)
    upper_t, lower_t = both_sides(lowered, 1, "ta", 1, lax.axis_size("ta"))
    stacked = jnp.stack(
        [lowered, upper_x, lower_x, upper_y, lower_y, upper_z, lower_z, upper_t, lower_t], 2
    )
    half_width = lowered.shape[-1] // 2
    real_part = stacked[..., :half_width]
    imag_part = stacked[..., half_width:]
    real_input = jnp.concatenate([real_part, -imag_part], -1)
    imag_input = jnp.concatenate([imag_part, real_part], -1)
    inputs = jnp.stack([real_input, imag_input], 0)
    result = jnp.einsum(
        "tbzyxdik,pntdbzyxk->pntbzyxi", coarse_links, inputs, preferred_element_type=jnp.float32
    )
    return jnp.concatenate([result[0], result[1]], -1)


def precondition(vector_in, null_vectors, coarse_inverse):
    lowered = vector_in.astype(jnp.bfloat16)
    coarse = jnp.einsum(
        "tbzyxjk,ntbzyxk->nj", null_vectors, lowered, preferred_element_type=jnp.float32
    ).astype(jnp.bfloat16)
    inverse_rows = coarse_inverse[0]
    correction = lax.dot_general(
        gather_tiled(coarse, "xyz", 1),
        inverse_rows,
        (((1,), (1,)), ((), ())),
        preferred_element_type=jnp.float32,
    ).astype(jnp.bfloat16)
    prolonged = jnp.einsum(
        "tbzyxjk,nj->ntbzyxk", null_vectors, correction, preferred_element_type=jnp.float32
    )
    return OMEGA * vector_in + prolonged


def inner_rows(left_vec, right_vec):
    return jnp.sum(left_vec * right_vec, axis=(1, 2, 3, 4, 5, 6))


def scaled(weights, vector_in):
    return weights[:, None, None, None, None, None, None] * vector_in


def pair_products(image, residual):
    both = total_sum(jnp.stack([inner_rows(image, image), inner_rows(image, residual)]))
    return (both[0], both[1])


def shards(right_side, coarse_links, null_vectors, coarse_inverse):
    residual = right_side
    direction_a = precondition(residual, null_vectors, coarse_inverse)
    image_a = apply_links(coarse_links, direction_a.astype(jnp.bfloat16))
    norm_a, correlation_a = pair_products(image_a, residual)
    step_a = correlation_a / (norm_a + EPS)
    solution = scaled(step_a, direction_a)
    residual = residual - scaled(step_a, image_a)
    direction_b = precondition(residual, null_vectors, coarse_inverse)
    image_b = apply_links(coarse_links, direction_b.astype(jnp.bfloat16))
    sums = total_sum(
        jnp.stack(
            [
                inner_rows(image_a, image_b),
                inner_rows(image_b, image_b),
                inner_rows(image_b, residual),
                inner_rows(image_a, residual),
            ]
        )
    )
    projection_sum, square_b, raw_correlation, shared_correlation = (
        sums[0], sums[1], sums[2], sums[3]
    )
    beta_coef = projection_sum / (norm_a + EPS)
    image_b = image_b - scaled(beta_coef, image_a)
    direction_b = direction_b - scaled(beta_coef, direction_a)
    norm_b = jnp.maximum(
        square_b - beta_coef * (2.0 * projection_sum - beta_coef * norm_a), 0.0
    )
    correlation_b = raw_correlation - beta_coef * shared_correlation
    step_b = correlation_b / (norm_b + EPS)
    solution = solution + scaled(step_b, direction_b)
    residual = residual - scaled(step_b, image_b)
    return (solution, residual)


def solution(mesh):
    in_specs = (
        P(None, "ta", "xyz", None, None, None, None),
        P("ta", "xyz", None, None, None, None, None, None),
        P("ta", "xyz", None, None, None, None, None),
        P("ta", "xyz", None),
    )
    out_specs = (
        P(None, "ta", "xyz", None, None, None, None),
        P(None, "ta", "xyz", None, None, None, None),
    )
    return jax.shard_map(shards, mesh=mesh, in_specs=in_specs, out_specs=out_specs, check_vma=False)
```

```python
import jax
import jax.numpy as jnp
from jax import lax
from jax.sharding import PartitionSpec as P

OMEGA = 0.4
EPS = 1e-06


def is_power_of_two(count):
    return count & (count - 1) == 0


def exchange(x, axis, bit):
    count = lax.axis_size(axis)
    return lax.ppermute(x, axis, [(i, i ^ bit) for i in range(count)])


def shifted(x, axis, shift):
    count = lax.axis_size(axis)
    return lax.ppermute(x, axis, [(i, (i + shift) % count) for i in range(count)])


def axis_sum(x, axis):
    count = lax.axis_size(axis)
    if count <= 8:
        received = [shifted(x, axis, shift) for shift in range(1, count)]
        for part in received:
            x = x + part
        return x
    if not is_power_of_two(count):
        return lax.psum(x, axis)
    bit = 1
    while bit < count:
        x = x + exchange(x, axis, bit)
        bit *= 2
    return x


def total_sum(x):
    return axis_sum(axis_sum(x, "xyz"), "ta")


def gather_tiled(x, axis, dim):
    count = lax.axis_size(axis)
    if not is_power_of_two(count):
        return lax.all_gather(x, axis, axis=dim, tiled=True)
    me = lax.axis_index(axis)
    bit = 1
    while bit < count:
        other = exchange(x, axis, bit)
        x = jnp.where(
            me // bit % 2 == 0,
            jnp.concatenate([x, other], dim),
            jnp.concatenate([other, x], dim),
        )
        bit *= 2
    return x


def neighbour_source(device, stride, extent, step):
    coord = device // stride % extent
    return device + ((coord + step) % extent - coord) * stride


def both_sides(lowered, which, axis, stride, extent):
    length = lowered.shape[which]
    count = lax.axis_size(axis)
    first = lax.slice_in_dim(lowered, 0, 1, axis=which)
    last = lax.slice_in_dim(lowered, length - 1, length, axis=which)
    if extent == 1:
        from_upper, from_lower = first, last
    elif extent == 2:
        perm = [(neighbour_source(d, stride, extent, 1), d) for d in range(count)]
        if length == 1:
            from_upper = from_lower = lax.ppermute(first, axis, perm)
        else:
            pair = lax.ppermute(jnp.concatenate([first, last], which), axis, perm)
            from_upper = lax.slice_in_dim(pair, 0, 1, axis=which)
            from_lower = lax.slice_in_dim(pair, 1, 2, axis=which)
    else:
        up = [(neighbour_source(d, stride, extent, 1), d) for d in range(count)]
        down = [(neighbour_source(d, stride, extent, -1), d) for d in range(count)]
        from_upper = lax.ppermute(first, axis, up)
        from_lower = lax.ppermute(last, axis, down)
    upper = jnp.concatenate([lax.slice_in_dim(lowered, 1, length, axis=which), from_upper], which)
    lower = jnp.concatenate(
        [from_lower, lax.slice_in_dim(lowered, 0, length - 1, axis=which)], which
    )
    return (upper, lower)


def apply_links(coarse_links, lowered):
    blocks_total = lax.axis_size("xyz")
    across_x = 2 + 2 * min(blocks_total // 64, 1)
    across_z = blocks_total // (across_x * across_x)
    upper_x, lower_x = both_sides(lowered, 5, "xyz", 1, across_x)
    upper_y, lower_y = both_sides(lowered, 4, "xyz", across_x, across_x)
    upper_z, lower_z = both_sides(lowered, 3, "xyz", across_x * across_x, across_z)
    upper_t, lower_t = both_sides(lowered, 1, "ta", 1, lax.axis_size("ta"))
    stacked = jnp.stack(
        [lowered, upper_x, lower_x, upper_y, lower_y, upper_z, lower_z, upper_t, lower_t], 2
    )
    half_width = lowered.shape[-1] // 2
    real_part = stacked[..., :half_width]
    imag_part = stacked[..., half_width:]
    real_input = jnp.concatenate([real_part, -imag_part], -1)
    imag_input = jnp.concatenate([imag_part, real_part], -1)
    inputs = jnp.stack([real_input, imag_input], 0)
    result = jnp.einsum(
        "tbzyxdik,pntdbzyxk->pntbzyxi", coarse_links, inputs, preferred_element_type=jnp.float32
    )
    return jnp.concatenate([result[0], result[1]], -1)


def precondition(vector_in, null_vectors, coarse_inverse):
    lowered = vector_in.astype(jnp.bfloat16)
    coarse = jnp.einsum(
        "tbzyxjk,ntbzyxk->nj", null_vectors, lowered, preferred_element_type=jnp.float32
    ).astype(jnp.bfloat16)
    inverse_rows = coarse_inverse[0]
    count = lax.axis_size("xyz")
    if count <= 8:
        width = coarse.shape[1]
        me = lax.axis_index("xyz")
        blocks = [coarse] + [shifted(coarse, "xyz", -shift) for shift in range(1, count)]
        gathered = jnp.concatenate(blocks, 1)
        doubled = jnp.concatenate([inverse_rows, inverse_rows], 1)
        inverse_rows = lax.dynamic_slice_in_dim(doubled, me * width, count * width, axis=1)
    else:
        gathered = gather_tiled(coarse, "xyz", 1)
    correction = lax.dot_general(
        gathered,
        inverse_rows,
        (((1,), (1,)), ((), ())),
        preferred_element_type=jnp.float32,
    ).astype(jnp.bfloat16)
    prolonged = jnp.einsum(
        "tbzyxjk,nj->ntbzyxk", null_vectors, correction, preferred_element_type=jnp.float32
    )
    return OMEGA * vector_in + prolonged


def inner_rows(left_vec, right_vec):
    return jnp.sum(left_vec * right_vec, axis=(1, 2, 3, 4, 5, 6))


def scaled(weights, vector_in):
    return weights[:, None, None, None, None, None, None] * vector_in


def pair_products(image, residual):
    both = total_sum(jnp.stack([inner_rows(image, image), inner_rows(image, residual)]))
    return (both[0], both[1])


def shards(right_side, coarse_links, null_vectors, coarse_inverse):
    residual = right_side
    direction_a = precondition(residual, null_vectors, coarse_inverse)
    image_a = apply_links(coarse_links, direction_a.astype(jnp.bfloat16))
    norm_a, correlation_a = pair_products(image_a, residual)
    step_a = correlation_a / (norm_a + EPS)
    solution = scaled(step_a, direction_a)
    residual = residual - scaled(step_a, image_a)
    direction_b = precondition(residual, null_vectors, coarse_inverse)
    image_b = apply_links(coarse_links, direction_b.astype(jnp.bfloat16))
    sums = total_sum(
        jnp.stack(
            [
                inner_rows(image_a, image_b),
                inner_rows(image_b, image_b),
                inner_rows(image_b, residual),
                inner_rows(image_a, residual),
            ]
        )
    )
    projection_sum, square_b, raw_correlation, shared_correlation = (
        sums[0], sums[1], sums[2], sums[3]
    )
    beta_coef = projection_sum / (norm_a + EPS)
    image_b = image_b - scaled(beta_coef, image_a)
    direction_b = direction_b - scaled(beta_coef, direction_a)
    norm_b = jnp.maximum(
        square_b - beta_coef * (2.0 * projection_sum - beta_coef * norm_a), 0.0
    )
    correlation_b = raw_correlation - beta_coef * shared_correlation
    step_b = correlation_b / (norm_b + EPS)
    solution = solution + scaled(step_b, direction_b)
    residual = residual - scaled(step_b, image_b)
    return (solution, residual)


def solution(mesh):
    in_specs = (
        P(None, "ta", "xyz", None, None, None, None),
        P("ta", "xyz", None, None, None, None, None, None),
        P("ta", "xyz", None, None, None, None, None),
        P("ta", "xyz", None),
    )
    out_specs = (
        P(None, "ta", "xyz", None, None, None, None),
        P(None, "ta", "xyz", None, None, None, None),
    )
    return jax.shard_map(shards, mesh=mesh, in_specs=in_specs, out_specs=out_specs, check_vma=False)
```

```python
import jax
import jax.numpy as jnp
from jax import lax
from jax.sharding import PartitionSpec as P

OMEGA = 0.4
EPS = 1e-06


def is_power_of_two(count):
    return count & (count - 1) == 0


def exchange(x, axis, bit):
    count = lax.axis_size(axis)
    return lax.ppermute(x, axis, [(i, i ^ bit) for i in range(count)])


def axis_sum(x, axis):
    count = lax.axis_size(axis)
    if not is_power_of_two(count):
        return lax.psum(x, axis)
    bit = 1
    while bit < count:
        x = x + exchange(x, axis, bit)
        bit *= 2
    return x


def total_sum(x):
    axes = ("ta", "xyz")
    count = lax.axis_size("ta") * lax.axis_size("xyz")
    copies = jnp.broadcast_to(x[None], (count,) + x.shape)
    return jnp.sum(lax.all_to_all(copies, axes, 0, 0), axis=0)


def gather_tiled(x, axis, dim):
    count = lax.axis_size(axis)
    copies = jnp.broadcast_to(x[None], (count,) + x.shape)
    parts = lax.all_to_all(copies, axis, 0, 0)
    return jnp.concatenate([parts[i] for i in range(count)], dim)


def neighbour_source(device, stride, extent, step):
    coord = device // stride % extent
    return device + ((coord + step) % extent - coord) * stride


def both_sides(lowered, which, axis, stride, extent):
    length = lowered.shape[which]
    count = lax.axis_size(axis)
    first = lax.slice_in_dim(lowered, 0, 1, axis=which)
    last = lax.slice_in_dim(lowered, length - 1, length, axis=which)
    if extent == 1:
        from_upper, from_lower = first, last
    elif extent == 2:
        perm = [(neighbour_source(d, stride, extent, 1), d) for d in range(count)]
        if length == 1:
            from_upper = from_lower = lax.ppermute(first, axis, perm)
        else:
            pair = lax.ppermute(jnp.concatenate([first, last], which), axis, perm)
            from_upper = lax.slice_in_dim(pair, 0, 1, axis=which)
            from_lower = lax.slice_in_dim(pair, 1, 2, axis=which)
    else:
        up = [(neighbour_source(d, stride, extent, 1), d) for d in range(count)]
        down = [(neighbour_source(d, stride, extent, -1), d) for d in range(count)]
        from_upper = lax.ppermute(first, axis, up)
        from_lower = lax.ppermute(last, axis, down)
    upper = jnp.concatenate([lax.slice_in_dim(lowered, 1, length, axis=which), from_upper], which)
    lower = jnp.concatenate(
        [from_lower, lax.slice_in_dim(lowered, 0, length - 1, axis=which)], which
    )
    return (upper, lower)


def apply_links(coarse_links, lowered):
    blocks_total = lax.axis_size("xyz")
    across_x = 2 + 2 * min(blocks_total // 64, 1)
    across_z = blocks_total // (across_x * across_x)
    upper_x, lower_x = both_sides(lowered, 5, "xyz", 1, across_x)
    upper_y, lower_y = both_sides(lowered, 4, "xyz", across_x, across_x)
    upper_z, lower_z = both_sides(lowered, 3, "xyz", across_x * across_x, across_z)
    upper_t, lower_t = both_sides(lowered, 1, "ta", 1, lax.axis_size("ta"))
    stacked = jnp.stack(
        [lowered, upper_x, lower_x, upper_y, lower_y, upper_z, lower_z, upper_t, lower_t], 2
    )
    half_width = lowered.shape[-1] // 2
    real_part = stacked[..., :half_width]
    imag_part = stacked[..., half_width:]
    real_input = jnp.concatenate([real_part, -imag_part], -1)
    imag_input = jnp.concatenate([imag_part, real_part], -1)
    inputs = jnp.stack([real_input, imag_input], 0)
    result = jnp.einsum(
        "tbzyxdik,pntdbzyxk->pntbzyxi", coarse_links, inputs, preferred_element_type=jnp.float32
    )
    return jnp.concatenate([result[0], result[1]], -1)


def precondition(vector_in, null_vectors, coarse_inverse):
    lowered = vector_in.astype(jnp.bfloat16)
    coarse = jnp.einsum(
        "tbzyxjk,ntbzyxk->nj", null_vectors, lowered, preferred_element_type=jnp.float32
    ).astype(jnp.bfloat16)
    inverse_rows = coarse_inverse[0]
    correction = lax.dot_general(
        gather_tiled(coarse, "xyz", 1),
        inverse_rows,
        (((1,), (1,)), ((), ())),
        preferred_element_type=jnp.float32,
    ).astype(jnp.bfloat16)
    prolonged = jnp.einsum(
        "tbzyxjk,nj->ntbzyxk", null_vectors, correction, preferred_element_type=jnp.float32
    )
    return OMEGA * vector_in + prolonged


def inner_rows(left_vec, right_vec):
    return jnp.sum(left_vec * right_vec, axis=(1, 2, 3, 4, 5, 6))


def scaled(weights, vector_in):
    return weights[:, None, None, None, None, None, None] * vector_in


def pair_products(image, residual):
    both = total_sum(jnp.stack([inner_rows(image, image), inner_rows(image, residual)]))
    return (both[0], both[1])


def shards(right_side, coarse_links, null_vectors, coarse_inverse):
    residual = right_side
    direction_a = precondition(residual, null_vectors, coarse_inverse)
    image_a = apply_links(coarse_links, direction_a.astype(jnp.bfloat16))
    norm_a, correlation_a = pair_products(image_a, residual)
    step_a = correlation_a / (norm_a + EPS)
    solution = scaled(step_a, direction_a)
    residual = residual - scaled(step_a, image_a)
    direction_b = precondition(residual, null_vectors, coarse_inverse)
    image_b = apply_links(coarse_links, direction_b.astype(jnp.bfloat16))
    sums = total_sum(
        jnp.stack(
            [
                inner_rows(image_a, image_b),
                inner_rows(image_b, image_b),
                inner_rows(image_b, residual),
                inner_rows(image_a, residual),
            ]
        )
    )
    projection_sum, square_b, raw_correlation, shared_correlation = (
        sums[0], sums[1], sums[2], sums[3]
    )
    beta_coef = projection_sum / (norm_a + EPS)
    image_b = image_b - scaled(beta_coef, image_a)
    direction_b = direction_b - scaled(beta_coef, direction_a)
    norm_b = jnp.maximum(
        square_b - beta_coef * (2.0 * projection_sum - beta_coef * norm_a), 0.0
    )
    correlation_b = raw_correlation - beta_coef * shared_correlation
    step_b = correlation_b / (norm_b + EPS)
    solution = solution + scaled(step_b, direction_b)
    residual = residual - scaled(step_b, image_b)
    return (solution, residual)


def solution(mesh):
    in_specs = (
        P(None, "ta", "xyz", None, None, None, None),
        P("ta", "xyz", None, None, None, None, None, None),
        P("ta", "xyz", None, None, None, None, None),
        P("ta", "xyz", None),
    )
    out_specs = (
        P(None, "ta", "xyz", None, None, None, None),
        P(None, "ta", "xyz", None, None, None, None),
    )
    return jax.shard_map(shards, mesh=mesh, in_specs=in_specs, out_specs=out_specs, check_vma=False)
```

```python
import jax
import jax.numpy as jnp
from jax import lax
from jax.sharding import PartitionSpec as P

OMEGA = 0.4
EPS = 1e-06


def total_sum(x):
    axes = ("ta", "xyz")
    count = lax.axis_size("ta") * lax.axis_size("xyz")
    copies = jnp.broadcast_to(x[None], (count,) + x.shape)
    return jnp.sum(lax.all_to_all(copies, axes, 0, 0), axis=0)


def neighbour_source(device, stride, extent, step):
    coord = device // stride % extent
    return device + ((coord + step) % extent - coord) * stride


def neighbour_plan():
    blocks_total = lax.axis_size("xyz")
    across_x = 2 + 2 * min(blocks_total // 64, 1)
    across_z = blocks_total // (across_x * across_x)
    specs = (
        (5, "xyz", 1, across_x),
        (4, "xyz", across_x, across_x),
        (3, "xyz", across_x * across_x, across_z),
        (1, "ta", 1, lax.axis_size("ta")),
    )
    directions = []
    for dim, axis, stride, extent in specs:
        count = lax.axis_size(axis)
        for step in (1, -1):
            perm = tuple((neighbour_source(d, stride, extent, step), d) for d in range(count))
            directions.append((dim, axis, step, perm))
    groups = {}
    order = []
    for k, (dim, axis, step, perm) in enumerate(directions):
        key = (axis, perm)
        if key not in groups:
            groups[key] = []
            order.append(key)
        groups[key].append(k)
    return directions, [(key, groups[key]) for key in order]


def face_of(x, dim, step):
    index = 0 if step > 0 else x.shape[dim] - 1
    return lax.slice_in_dim(x, index, index + 1, axis=dim)


def swap(axis, perm, arrays):
    width = arrays[0].shape[-1]
    flat = jnp.concatenate([a.reshape(-1, width) for a in arrays], 0)
    if any(s != d for s, d in perm):
        flat = lax.ppermute(flat, axis, list(perm))
    out, row = [], 0
    for a in arrays:
        rows = a.size // width
        out.append(flat[row : row + rows].reshape(a.shape))
        row += rows
    return out


def exchange_fields(plan, field):
    directions, groups = plan
    received = [None] * len(directions)
    for (axis, perm), members in groups:
        faces = [face_of(field, directions[k][0], directions[k][2]) for k in members]
        for k, got in zip(members, swap(axis, perm, faces)):
            received[k] = got
    return received


def exchange_static(plan, null_vectors, inverse_rows):
    directions, groups = plan
    nulls = [None] * len(directions)
    rows = [None] * len(directions)
    for (axis, perm), members in groups:
        faces = [face_of(null_vectors, directions[k][0] - 1, directions[k][2]) for k in members]
        got = swap(axis, perm, faces + [inverse_rows])
        for k, null_face in zip(members, got[:-1]):
            nulls[k] = null_face
            rows[k] = got[-1]
    return nulls, rows


def correct(slab, rows):
    return lax.dot_general(
        slab, rows, (((1,), (1,)), ((), ())), preferred_element_type=jnp.float32
    ).astype(jnp.bfloat16)


def prolong(null_vectors, correction):
    return jnp.einsum(
        "tbzyxjk,nj->ntbzyxk", null_vectors, correction, preferred_element_type=jnp.float32
    )


def precondition(plan, vector_in, faces_in, null_vectors, inverse_rows, static):
    directions, _ = plan
    nulls, rows = static
    lowered = vector_in.astype(jnp.bfloat16)
    coarse = jnp.einsum(
        "tbzyxjk,ntbzyxk->nj", null_vectors, lowered, preferred_element_type=jnp.float32
    ).astype(jnp.bfloat16)
    slabs_total = lax.axis_size("ta")
    blocks_total = lax.axis_size("xyz")
    count, width = coarse.shape
    me = lax.axis_index("ta")

    def joined(slab):
        return jnp.transpose(slab, (1, 0, 2)).reshape(count, blocks_total * width)

    if slabs_total * blocks_total <= 64:
        copies = jnp.broadcast_to(coarse[None], (slabs_total * blocks_total, count, width))
        parts = lax.all_to_all(copies, ("ta", "xyz"), 0, 0)
        slabs = parts.reshape(slabs_total, blocks_total, count, width)
        slab_for = {
            step: joined(
                lax.dynamic_index_in_dim(slabs, (me + step) % slabs_total, 0, keepdims=False)
            )
            for step in (0, 1, -1)
        }
    else:
        copies = jnp.broadcast_to(coarse[None], (blocks_total, count, width))
        own = joined(lax.all_to_all(copies, "xyz", 0, 0))
        slab_for = {0: own}
        for step in (1, -1):
            perm = [(neighbour_source(d, 1, slabs_total, step), d) for d in range(slabs_total)]
            slab_for[step] = lax.ppermute(own, "ta", perm)
    own_slab = slab_for[0]
    direction = OMEGA * vector_in + prolong(null_vectors, correct(own_slab, inverse_rows))
    faces = []
    for k, (dim, axis, step, perm) in enumerate(directions):
        slab = own_slab if axis == "xyz" else slab_for[step]
        face = OMEGA * faces_in[k] + prolong(nulls[k], correct(slab, rows[k]))
        faces.append(face.astype(jnp.bfloat16))
    return direction, faces


def apply_links(plan, coarse_links, lowered, faces):
    directions, _ = plan
    shifted = [lowered]
    for k, (dim, axis, step, perm) in enumerate(directions):
        length = lowered.shape[dim]
        if step > 0:
            parts = [lax.slice_in_dim(lowered, 1, length, axis=dim), faces[k]]
        else:
            parts = [faces[k], lax.slice_in_dim(lowered, 0, length - 1, axis=dim)]
        shifted.append(jnp.concatenate(parts, dim))
    stacked = jnp.stack(shifted, 2)
    half_width = lowered.shape[-1] // 2
    real_part = stacked[..., :half_width]
    imag_part = stacked[..., half_width:]
    real_input = jnp.concatenate([real_part, -imag_part], -1)
    imag_input = jnp.concatenate([imag_part, real_part], -1)
    inputs = jnp.stack([real_input, imag_input], 0)
    result = jnp.einsum(
        "tbzyxdik,pntdbzyxk->pntbzyxi", coarse_links, inputs, preferred_element_type=jnp.float32
    )
    return jnp.concatenate([result[0], result[1]], -1)


def inner_rows(left_vec, right_vec):
    return jnp.sum(left_vec * right_vec, axis=(1, 2, 3, 4, 5, 6))


def scaled(weights, vector_in):
    return weights[:, None, None, None, None, None, None] * vector_in


def pair_products(image, residual):
    both = total_sum(jnp.stack([inner_rows(image, image), inner_rows(image, residual)]))
    return (both[0], both[1])


def shards(right_side, coarse_links, null_vectors, coarse_inverse):
    plan = neighbour_plan()
    inverse_rows = coarse_inverse[0]
    static = exchange_static(plan, null_vectors, inverse_rows)
    residual = right_side
    residual_faces = exchange_fields(plan, residual)
    direction_a, faces_a = precondition(
        plan, residual, residual_faces, null_vectors, inverse_rows, static
    )
    image_a = apply_links(plan, coarse_links, direction_a.astype(jnp.bfloat16), faces_a)
    image_faces = exchange_fields(plan, image_a)
    norm_a, correlation_a = pair_products(image_a, residual)
    step_a = correlation_a / (norm_a + EPS)
    solution = scaled(step_a, direction_a)
    residual = residual - scaled(step_a, image_a)
    residual_faces = [
        face - scaled(step_a, image_face)
        for face, image_face in zip(residual_faces, image_faces)
    ]
    direction_b, faces_b = precondition(
        plan, residual, residual_faces, null_vectors, inverse_rows, static
    )
    image_b = apply_links(plan, coarse_links, direction_b.astype(jnp.bfloat16), faces_b)
    sums = total_sum(
        jnp.stack(
            [
                inner_rows(image_a, image_b),
                inner_rows(image_b, image_b),
                inner_rows(image_b, residual),
                inner_rows(image_a, residual),
            ]
        )
    )
    projection_sum, square_b, raw_correlation, shared_correlation = (
        sums[0], sums[1], sums[2], sums[3]
    )
    beta_coef = projection_sum / (norm_a + EPS)
    image_b = image_b - scaled(beta_coef, image_a)
    direction_b = direction_b - scaled(beta_coef, direction_a)
    norm_b = jnp.maximum(
        square_b - beta_coef * (2.0 * projection_sum - beta_coef * norm_a), 0.0
    )
    correlation_b = raw_correlation - beta_coef * shared_correlation
    step_b = correlation_b / (norm_b + EPS)
    solution = solution + scaled(step_b, direction_b)
    residual = residual - scaled(step_b, image_b)
    return (solution, residual)


def solution(mesh):
    in_specs = (
        P(None, "ta", "xyz", None, None, None, None),
        P("ta", "xyz", None, None, None, None, None, None),
        P("ta", "xyz", None, None, None, None, None),
        P("ta", "xyz", None),
    )
    out_specs = (
        P(None, "ta", "xyz", None, None, None, None),
        P(None, "ta", "xyz", None, None, None, None),
    )
    return jax.shard_map(shards, mesh=mesh, in_specs=in_specs, out_specs=out_specs, check_vma=False)
```

```python
import jax
import jax.numpy as jnp
from jax import lax
from jax.sharding import PartitionSpec as P

OMEGA = 0.4
EPS = 1e-06


def is_power_of_two(count):
    return count & (count - 1) == 0


def exchange(x, axis, bit):
    count = lax.axis_size(axis)
    return lax.ppermute(x, axis, [(i, i ^ bit) for i in range(count)])


def axis_sum(x, axis):
    count = lax.axis_size(axis)
    if not is_power_of_two(count):
        return lax.psum(x, axis)
    bit = 1
    while bit < count:
        x = x + exchange(x, axis, bit)
        bit *= 2
    return x


def total_sum(x):
    axes = ("ta", "xyz")
    count = lax.axis_size("ta") * lax.axis_size("xyz")
    copies = jnp.broadcast_to(x[None], (count,) + x.shape)
    return jnp.sum(lax.all_to_all(copies, axes, 0, 0), axis=0)


def neighbour_source(device, stride, extent, step):
    coord = device // stride % extent
    return device + ((coord + step) % extent - coord) * stride


def both_sides(lowered, which, axis, stride, extent):
    length = lowered.shape[which]
    count = lax.axis_size(axis)
    first = lax.slice_in_dim(lowered, 0, 1, axis=which)
    last = lax.slice_in_dim(lowered, length - 1, length, axis=which)
    if extent == 1:
        from_upper, from_lower = first, last
    elif extent == 2:
        perm = [(neighbour_source(d, stride, extent, 1), d) for d in range(count)]
        if length == 1:
            from_upper = from_lower = lax.ppermute(first, axis, perm)
        else:
            pair = lax.ppermute(jnp.concatenate([first, last], which), axis, perm)
            from_upper = lax.slice_in_dim(pair, 0, 1, axis=which)
            from_lower = lax.slice_in_dim(pair, 1, 2, axis=which)
    else:
        up = [(neighbour_source(d, stride, extent, 1), d) for d in range(count)]
        down = [(neighbour_source(d, stride, extent, -1), d) for d in range(count)]
        from_upper = lax.ppermute(first, axis, up)
        from_lower = lax.ppermute(last, axis, down)
    upper = jnp.concatenate([lax.slice_in_dim(lowered, 1, length, axis=which), from_upper], which)
    lower = jnp.concatenate(
        [from_lower, lax.slice_in_dim(lowered, 0, length - 1, axis=which)], which
    )
    return (upper, lower)


def apply_links(coarse_links, lowered):
    blocks_total = lax.axis_size("xyz")
    across_x = 2 + 2 * min(blocks_total // 64, 1)
    across_z = blocks_total // (across_x * across_x)
    upper_x, lower_x = both_sides(lowered, 5, "xyz", 1, across_x)
    upper_y, lower_y = both_sides(lowered, 4, "xyz", across_x, across_x)
    upper_z, lower_z = both_sides(lowered, 3, "xyz", across_x * across_x, across_z)
    upper_t, lower_t = both_sides(lowered, 1, "ta", 1, lax.axis_size("ta"))
    stacked = jnp.stack(
        [lowered, upper_x, lower_x, upper_y, lower_y, upper_z, lower_z, upper_t, lower_t], 2
    )
    half_width = lowered.shape[-1] // 2
    real_part = stacked[..., :half_width]
    imag_part = stacked[..., half_width:]
    real_input = jnp.concatenate([real_part, -imag_part], -1)
    imag_input = jnp.concatenate([imag_part, real_part], -1)
    inputs = jnp.stack([real_input, imag_input], 0)
    result = jnp.einsum(
        "tbzyxdik,pntdbzyxk->pntbzyxi", coarse_links, inputs, preferred_element_type=jnp.float32
    )
    return jnp.concatenate([result[0], result[1]], -1)


def restrict_exact(null_vectors, field):
    return jnp.einsum(
        "tbzyxjk,ntbzyxk->nj",
        null_vectors.astype(jnp.float32),
        field,
        preferred_element_type=jnp.float32,
        precision=lax.Precision.HIGHEST,
    )


def slab_columns(parts):
    return jnp.transpose(parts, (1, 0, 2)).reshape(parts.shape[1], -1)


def finish(vector_in, slab, null_vectors, inverse_rows):
    correction = lax.dot_general(
        slab,
        inverse_rows,
        (((1,), (1,)), ((), ())),
        preferred_element_type=jnp.float32,
    ).astype(jnp.bfloat16)
    prolonged = jnp.einsum(
        "tbzyxjk,nj->ntbzyxk", null_vectors, correction, preferred_element_type=jnp.float32
    )
    return OMEGA * vector_in + prolonged


def inner_rows(left_vec, right_vec):
    return jnp.sum(left_vec * right_vec, axis=(1, 2, 3, 4, 5, 6))


def scaled(weights, vector_in):
    return weights[:, None, None, None, None, None, None] * vector_in


def shards(right_side, coarse_links, null_vectors, coarse_inverse):
    inverse_rows = coarse_inverse[0]
    slabs_total = lax.axis_size("ta")
    blocks_total = lax.axis_size("xyz")
    residual = right_side
    coarse = jnp.einsum(
        "tbzyxjk,ntbzyxk->nj",
        null_vectors,
        residual.astype(jnp.bfloat16),
        preferred_element_type=jnp.float32,
    ).astype(jnp.bfloat16)
    width = coarse.shape[1]
    payload = jnp.concatenate(
        [coarse.astype(jnp.float32), restrict_exact(null_vectors, residual)], 1
    )
    parts = lax.all_to_all(
        jnp.broadcast_to(payload[None], (blocks_total,) + payload.shape), "xyz", 0, 0
    )
    slab_a = slab_columns(parts[:, :, :width]).astype(jnp.bfloat16)
    slab_residual = slab_columns(parts[:, :, width:])
    direction_a = finish(residual, slab_a, null_vectors, inverse_rows)
    image_a = apply_links(coarse_links, direction_a.astype(jnp.bfloat16))
    image_coarse = restrict_exact(null_vectors, image_a)
    pair_local = jnp.stack([inner_rows(image_a, image_a), inner_rows(image_a, residual)], 1)
    if slabs_total * blocks_total <= 64:
        local = jnp.concatenate([pair_local, image_coarse], 1)
        gathered = lax.all_to_all(
            jnp.broadcast_to(local[None], (slabs_total * blocks_total,) + local.shape),
            ("ta", "xyz"),
            0,
            0,
        )
        pair = jnp.sum(gathered[:, :, :2], axis=0)
        image_slabs = gathered[:, :, 2:].reshape(
            (slabs_total, blocks_total) + image_coarse.shape
        )
        slab_image = slab_columns(
            lax.dynamic_index_in_dim(image_slabs, lax.axis_index("ta"), 0, keepdims=False)
        )
    else:
        pair = total_sum(pair_local)
        slab_image = slab_columns(
            lax.all_to_all(
                jnp.broadcast_to(image_coarse[None], (blocks_total,) + image_coarse.shape),
                "xyz",
                0,
                0,
            )
        )
    norm_a, correlation_a = pair[:, 0], pair[:, 1]
    step_a = correlation_a / (norm_a + EPS)
    solution = scaled(step_a, direction_a)
    residual = residual - scaled(step_a, image_a)
    slab_b = (slab_residual - step_a[:, None] * slab_image).astype(jnp.bfloat16)
    direction_b = finish(residual, slab_b, null_vectors, inverse_rows)
    image_b = apply_links(coarse_links, direction_b.astype(jnp.bfloat16))
    sums = total_sum(
        jnp.stack(
            [
                inner_rows(image_a, image_b),
                inner_rows(image_b, image_b),
                inner_rows(image_b, residual),
                inner_rows(image_a, residual),
            ]
        )
    )
    projection_sum, square_b, raw_correlation, shared_correlation = (
        sums[0], sums[1], sums[2], sums[3]
    )
    beta_coef = projection_sum / (norm_a + EPS)
    image_b = image_b - scaled(beta_coef, image_a)
    direction_b = direction_b - scaled(beta_coef, direction_a)
    norm_b = jnp.maximum(
        square_b - beta_coef * (2.0 * projection_sum - beta_coef * norm_a), 0.0
    )
    correlation_b = raw_correlation - beta_coef * shared_correlation
    step_b = correlation_b / (norm_b + EPS)
    solution = solution + scaled(step_b, direction_b)
    residual = residual - scaled(step_b, image_b)
    return (solution, residual)


def solution(mesh):
    in_specs = (
        P(None, "ta", "xyz", None, None, None, None),
        P("ta", "xyz", None, None, None, None, None, None),
        P("ta", "xyz", None, None, None, None, None),
        P("ta", "xyz", None),
    )
    out_specs = (
        P(None, "ta", "xyz", None, None, None, None),
        P(None, "ta", "xyz", None, None, None, None),
    )
    return jax.shard_map(shards, mesh=mesh, in_specs=in_specs, out_specs=out_specs, check_vma=False)
```

```python
import jax
import jax.numpy as jnp
from jax import lax
from jax.sharding import PartitionSpec as P

OMEGA = 0.4
EPS = 1e-06


def is_power_of_two(count):
    return count & (count - 1) == 0


def exchange(x, axis, bit):
    count = lax.axis_size(axis)
    return lax.ppermute(x, axis, [(i, i ^ bit) for i in range(count)])


def axis_sum(x, axis):
    count = lax.axis_size(axis)
    if not is_power_of_two(count):
        return lax.psum(x, axis)
    bit = 1
    while bit < count:
        x = x + exchange(x, axis, bit)
        bit *= 2
    return x


def total_sum(x):
    axes = ("ta", "xyz")
    count = lax.axis_size("ta") * lax.axis_size("xyz")
    copies = jnp.broadcast_to(x[None], (count,) + x.shape)
    return jnp.sum(lax.all_to_all(copies, axes, 0, 0), axis=0)


def neighbour_source(device, stride, extent, step):
    coord = device // stride % extent
    return device + ((coord + step) % extent - coord) * stride


def both_sides(lowered, which, axis, stride, extent):
    length = lowered.shape[which]
    count = lax.axis_size(axis)
    first = lax.slice_in_dim(lowered, 0, 1, axis=which)
    last = lax.slice_in_dim(lowered, length - 1, length, axis=which)
    if extent == 1:
        from_upper, from_lower = first, last
    elif extent == 2:
        perm = [(neighbour_source(d, stride, extent, 1), d) for d in range(count)]
        if length == 1:
            from_upper = from_lower = lax.ppermute(first, axis, perm)
        else:
            pair = lax.ppermute(jnp.concatenate([first, last], which), axis, perm)
            from_upper = lax.slice_in_dim(pair, 0, 1, axis=which)
            from_lower = lax.slice_in_dim(pair, 1, 2, axis=which)
    else:
        up = [(neighbour_source(d, stride, extent, 1), d) for d in range(count)]
        down = [(neighbour_source(d, stride, extent, -1), d) for d in range(count)]
        from_upper = lax.ppermute(first, axis, up)
        from_lower = lax.ppermute(last, axis, down)
    upper = jnp.concatenate([lax.slice_in_dim(lowered, 1, length, axis=which), from_upper], which)
    lower = jnp.concatenate(
        [from_lower, lax.slice_in_dim(lowered, 0, length - 1, axis=which)], which
    )
    return (upper, lower)


def apply_links(coarse_links, lowered):
    blocks_total = lax.axis_size("xyz")
    across_x = 2 + 2 * min(blocks_total // 64, 1)
    across_z = blocks_total // (across_x * across_x)
    upper_x, lower_x = both_sides(lowered, 5, "xyz", 1, across_x)
    upper_y, lower_y = both_sides(lowered, 4, "xyz", across_x, across_x)
    upper_z, lower_z = both_sides(lowered, 3, "xyz", across_x * across_x, across_z)
    upper_t, lower_t = both_sides(lowered, 1, "ta", 1, lax.axis_size("ta"))
    stacked = jnp.stack(
        [lowered, upper_x, lower_x, upper_y, lower_y, upper_z, lower_z, upper_t, lower_t], 2
    )
    half_width = lowered.shape[-1] // 2
    real_part = stacked[..., :half_width]
    imag_part = stacked[..., half_width:]
    real_input = jnp.concatenate([real_part, -imag_part], -1)
    imag_input = jnp.concatenate([imag_part, real_part], -1)
    inputs = jnp.stack([real_input, imag_input], 0)
    result = jnp.einsum(
        "tbzyxdik,pntdbzyxk->pntbzyxi", coarse_links, inputs, preferred_element_type=jnp.float32
    )
    return jnp.concatenate([result[0], result[1]], -1)


def restrict_exact(null_vectors, field):
    return jnp.einsum(
        "tbzyxjk,ntbzyxk->jn",
        null_vectors.astype(jnp.float32),
        field,
        preferred_element_type=jnp.float32,
        precision=lax.Precision.HIGHEST,
    )


def finish(vector_in, slab, null_vectors, inverse_blocks):
    correction = lax.dot_general(
        slab,
        inverse_blocks,
        (((0, 1), (1, 2)), ((), ())),
        preferred_element_type=jnp.float32,
    ).astype(jnp.bfloat16)
    prolonged = jnp.einsum(
        "tbzyxjk,nj->ntbzyxk", null_vectors, correction, preferred_element_type=jnp.float32
    )
    return OMEGA * vector_in + prolonged


def inner_rows(left_vec, right_vec):
    return jnp.sum(left_vec * right_vec, axis=(1, 2, 3, 4, 5, 6))


def scaled(weights, vector_in):
    return weights[:, None, None, None, None, None, None] * vector_in


def shards(right_side, coarse_links, null_vectors, coarse_inverse):
    slabs_total = lax.axis_size("ta")
    blocks_total = lax.axis_size("xyz")
    inverse_rows = coarse_inverse[0]
    inverse_blocks = inverse_rows.reshape(
        inverse_rows.shape[0], blocks_total, inverse_rows.shape[1] // blocks_total
    )
    residual = right_side
    coarse = jnp.einsum(
        "tbzyxjk,ntbzyxk->jn",
        null_vectors,
        residual.astype(jnp.bfloat16),
        preferred_element_type=jnp.float32,
    ).astype(jnp.bfloat16)
    width = coarse.shape[0]
    payload = jnp.concatenate(
        [coarse.astype(jnp.float32), restrict_exact(null_vectors, residual)], 0
    )
    parts = lax.all_to_all(
        jnp.broadcast_to(payload[None], (blocks_total,) + payload.shape), "xyz", 0, 0
    )
    slab_a = parts[:, :width, :].astype(jnp.bfloat16)
    slab_residual = parts[:, width:, :]
    direction_a = finish(residual, slab_a, null_vectors, inverse_blocks)
    image_a = apply_links(coarse_links, direction_a.astype(jnp.bfloat16))
    image_coarse = restrict_exact(null_vectors, image_a)
    pair_local = jnp.stack([inner_rows(image_a, image_a), inner_rows(image_a, residual)], 0)
    if slabs_total * blocks_total <= 64:
        local = jnp.concatenate([pair_local, image_coarse], 0)
        gathered = lax.all_to_all(
            jnp.broadcast_to(local[None], (slabs_total * blocks_total,) + local.shape),
            ("ta", "xyz"),
            0,
            0,
        )
        pair = jnp.sum(gathered[:, :2, :], axis=0)
        image_slabs = gathered[:, 2:, :].reshape(
            (slabs_total, blocks_total) + image_coarse.shape
        )
        slab_image = lax.dynamic_index_in_dim(
            image_slabs, lax.axis_index("ta"), 0, keepdims=False
        )
    else:
        pair = total_sum(pair_local)
        slab_image = lax.all_to_all(
            jnp.broadcast_to(image_coarse[None], (blocks_total,) + image_coarse.shape),
            "xyz",
            0,
            0,
        )
    norm_a, correlation_a = pair[0], pair[1]
    step_a = correlation_a / (norm_a + EPS)
    solution = scaled(step_a, direction_a)
    residual = residual - scaled(step_a, image_a)
    slab_b = (slab_residual - step_a[None, None, :] * slab_image).astype(jnp.bfloat16)
    direction_b = finish(residual, slab_b, null_vectors, inverse_blocks)
    image_b = apply_links(coarse_links, direction_b.astype(jnp.bfloat16))
    sums = total_sum(
        jnp.stack(
            [
                inner_rows(image_a, image_b),
                inner_rows(image_b, image_b),
                inner_rows(image_b, residual),
                inner_rows(image_a, residual),
            ]
        )
    )
    projection_sum, square_b, raw_correlation, shared_correlation = (
        sums[0], sums[1], sums[2], sums[3]
    )
    beta_coef = projection_sum / (norm_a + EPS)
    image_b = image_b - scaled(beta_coef, image_a)
    direction_b = direction_b - scaled(beta_coef, direction_a)
    norm_b = jnp.maximum(
        square_b - beta_coef * (2.0 * projection_sum - beta_coef * norm_a), 0.0
    )
    correlation_b = raw_correlation - beta_coef * shared_correlation
    step_b = correlation_b / (norm_b + EPS)
    solution = solution + scaled(step_b, direction_b)
    residual = residual - scaled(step_b, image_b)
    return (solution, residual)


def solution(mesh):
    in_specs = (
        P(None, "ta", "xyz", None, None, None, None),
        P("ta", "xyz", None, None, None, None, None, None),
        P("ta", "xyz", None, None, None, None, None),
        P("ta", "xyz", None),
    )
    out_specs = (
        P(None, "ta", "xyz", None, None, None, None),
        P(None, "ta", "xyz", None, None, None, None),
    )
    return jax.shard_map(shards, mesh=mesh, in_specs=in_specs, out_specs=out_specs, check_vma=False)
```

```python
import jax
import jax.numpy as jnp
from jax import lax
from jax.sharding import PartitionSpec as P

OMEGA = 0.4
EPS = 1e-06


def is_power_of_two(count):
    return count & (count - 1) == 0


def exchange(x, axis, bit):
    count = lax.axis_size(axis)
    return lax.ppermute(x, axis, [(i, i ^ bit) for i in range(count)])


def axis_sum(x, axis):
    count = lax.axis_size(axis)
    if not is_power_of_two(count):
        return lax.psum(x, axis)
    bit = 1
    while bit < count:
        x = x + exchange(x, axis, bit)
        bit *= 2
    return x


def total_sum(x):
    axes = ("ta", "xyz")
    count = lax.axis_size("ta") * lax.axis_size("xyz")
    copies = jnp.broadcast_to(x[None], (count,) + x.shape)
    return jnp.sum(lax.all_to_all(copies, axes, 0, 0), axis=0)


def neighbour_source(device, stride, extent, step):
    coord = device // stride % extent
    return device + ((coord + step) % extent - coord) * stride


def both_sides(lowered, which, axis, stride, extent):
    length = lowered.shape[which]
    count = lax.axis_size(axis)
    first = lax.slice_in_dim(lowered, 0, 1, axis=which)
    last = lax.slice_in_dim(lowered, length - 1, length, axis=which)
    if extent == 1:
        from_upper, from_lower = first, last
    elif extent == 2:
        perm = [(neighbour_source(d, stride, extent, 1), d) for d in range(count)]
        if length == 1:
            from_upper = from_lower = lax.ppermute(first, axis, perm)
        else:
            pair = lax.ppermute(jnp.concatenate([first, last], which), axis, perm)
            from_upper = lax.slice_in_dim(pair, 0, 1, axis=which)
            from_lower = lax.slice_in_dim(pair, 1, 2, axis=which)
    else:
        up = [(neighbour_source(d, stride, extent, 1), d) for d in range(count)]
        down = [(neighbour_source(d, stride, extent, -1), d) for d in range(count)]
        from_upper = lax.ppermute(first, axis, up)
        from_lower = lax.ppermute(last, axis, down)
    upper = jnp.concatenate([lax.slice_in_dim(lowered, 1, length, axis=which), from_upper], which)
    lower = jnp.concatenate(
        [from_lower, lax.slice_in_dim(lowered, 0, length - 1, axis=which)], which
    )
    return (upper, lower)


def split_links(coarse_links):
    half_width = coarse_links.shape[-1] // 2
    real_part = coarse_links[..., :half_width]
    imag_part = coarse_links[..., half_width:]
    return jnp.stack(
        [
            jnp.concatenate([real_part, -imag_part], -1),
            jnp.concatenate([imag_part, real_part], -1),
        ],
        0,
    )


def apply_links(links_pair, lowered):
    blocks_total = lax.axis_size("xyz")
    across_x = 2 + 2 * min(blocks_total // 64, 1)
    across_z = blocks_total // (across_x * across_x)
    upper_x, lower_x = both_sides(lowered, 5, "xyz", 1, across_x)
    upper_y, lower_y = both_sides(lowered, 4, "xyz", across_x, across_x)
    upper_z, lower_z = both_sides(lowered, 3, "xyz", across_x * across_x, across_z)
    upper_t, lower_t = both_sides(lowered, 1, "ta", 1, lax.axis_size("ta"))
    stacked = jnp.stack(
        [lowered, upper_x, lower_x, upper_y, lower_y, upper_z, lower_z, upper_t, lower_t], 2
    )
    result = jnp.einsum(
        "ptbzyxdik,ntdbzyxk->pntbzyxi", links_pair, stacked, preferred_element_type=jnp.float32
    )
    return jnp.concatenate([result[0], result[1]], -1)


def restrict_exact(null_vectors, field):
    return jnp.einsum(
        "tbzyxjk,ntbzyxk->nj",
        null_vectors.astype(jnp.float32),
        field,
        preferred_element_type=jnp.float32,
        precision=lax.Precision.HIGHEST,
    )


def slab_columns(parts):
    return jnp.transpose(parts, (1, 0, 2)).reshape(parts.shape[1], -1)


def finish(vector_in, slab, null_vectors, inverse_rows):
    correction = lax.dot_general(
        slab,
        inverse_rows,
        (((1,), (1,)), ((), ())),
        preferred_element_type=jnp.float32,
    ).astype(jnp.bfloat16)
    prolonged = jnp.einsum(
        "tbzyxjk,nj->ntbzyxk", null_vectors, correction, preferred_element_type=jnp.float32
    )
    return OMEGA * vector_in + prolonged


def inner_rows(left_vec, right_vec):
    return jnp.sum(left_vec * right_vec, axis=(1, 2, 3, 4, 5, 6))


def scaled(weights, vector_in):
    return weights[:, None, None, None, None, None, None] * vector_in


def shards(right_side, coarse_links, null_vectors, coarse_inverse):
    inverse_rows = coarse_inverse[0]
    links_pair = split_links(coarse_links)
    slabs_total = lax.axis_size("ta")
    blocks_total = lax.axis_size("xyz")
    residual = right_side
    coarse = jnp.einsum(
        "tbzyxjk,ntbzyxk->nj",
        null_vectors,
        residual.astype(jnp.bfloat16),
        preferred_element_type=jnp.float32,
    ).astype(jnp.bfloat16)
    width = coarse.shape[1]
    payload = jnp.concatenate(
        [coarse.astype(jnp.float32), restrict_exact(null_vectors, residual)], 1
    )
    parts = lax.all_to_all(
        jnp.broadcast_to(payload[None], (blocks_total,) + payload.shape), "xyz", 0, 0
    )
    slab_a = slab_columns(parts[:, :, :width]).astype(jnp.bfloat16)
    slab_residual = slab_columns(parts[:, :, width:])
    direction_a = finish(residual, slab_a, null_vectors, inverse_rows)
    image_a = apply_links(links_pair, direction_a.astype(jnp.bfloat16))
    image_coarse = restrict_exact(null_vectors, image_a)
    pair_local = jnp.stack([inner_rows(image_a, image_a), inner_rows(image_a, residual)], 1)
    if slabs_total * blocks_total <= 64:
        local = jnp.concatenate([pair_local, image_coarse], 1)
        gathered = lax.all_to_all(
            jnp.broadcast_to(local[None], (slabs_total * blocks_total,) + local.shape),
            ("ta", "xyz"),
            0,
            0,
        )
        pair = jnp.sum(gathered[:, :, :2], axis=0)
        image_slabs = gathered[:, :, 2:].reshape(
            (slabs_total, blocks_total) + image_coarse.shape
        )
        slab_image = slab_columns(
            lax.dynamic_index_in_dim(image_slabs, lax.axis_index("ta"), 0, keepdims=False)
        )
    else:
        pair = total_sum(pair_local)
        slab_image = slab_columns(
            lax.all_to_all(
                jnp.broadcast_to(image_coarse[None], (blocks_total,) + image_coarse.shape),
                "xyz",
                0,
                0,
            )
        )
    norm_a, correlation_a = pair[:, 0], pair[:, 1]
    step_a = correlation_a / (norm_a + EPS)
    solution = scaled(step_a, direction_a)
    residual = residual - scaled(step_a, image_a)
    slab_b = (slab_residual - step_a[:, None] * slab_image).astype(jnp.bfloat16)
    direction_b = finish(residual, slab_b, null_vectors, inverse_rows)
    image_b = apply_links(links_pair, direction_b.astype(jnp.bfloat16))
    sums = total_sum(
        jnp.stack(
            [
                inner_rows(image_a, image_b),
                inner_rows(image_b, image_b),
                inner_rows(image_b, residual),
                inner_rows(image_a, residual),
            ]
        )
    )
    projection_sum, square_b, raw_correlation, shared_correlation = (
        sums[0], sums[1], sums[2], sums[3]
    )
    beta_coef = projection_sum / (norm_a + EPS)
    image_b = image_b - scaled(beta_coef, image_a)
    direction_b = direction_b - scaled(beta_coef, direction_a)
    norm_b = jnp.maximum(
        square_b - beta_coef * (2.0 * projection_sum - beta_coef * norm_a), 0.0
    )
    correlation_b = raw_correlation - beta_coef * shared_correlation
    step_b = correlation_b / (norm_b + EPS)
    solution = solution + scaled(step_b, direction_b)
    residual = residual - scaled(step_b, image_b)
    return (solution, residual)


def solution(mesh):
    in_specs = (
        P(None, "ta", "xyz", None, None, None, None),
        P("ta", "xyz", None, None, None, None, None, None),
        P("ta", "xyz", None, None, None, None, None),
        P("ta", "xyz", None),
    )
    out_specs = (
        P(None, "ta", "xyz", None, None, None, None),
        P(None, "ta", "xyz", None, None, None, None),
    )
    return jax.shard_map(shards, mesh=mesh, in_specs=in_specs, out_specs=out_specs, check_vma=False)
```

```python
import jax
import jax.numpy as jnp
from jax import lax
from jax.sharding import PartitionSpec as P

OMEGA = 0.4
EPS = 1e-06


def is_power_of_two(count):
    return count & (count - 1) == 0


def exchange(x, axis, bit):
    count = lax.axis_size(axis)
    return lax.ppermute(x, axis, [(i, i ^ bit) for i in range(count)])


def axis_sum(x, axis):
    count = lax.axis_size(axis)
    if not is_power_of_two(count):
        return lax.psum(x, axis)
    bit = 1
    while bit < count:
        x = x + exchange(x, axis, bit)
        bit *= 2
    return x


def total_sum(x):
    axes = ("ta", "xyz")
    count = lax.axis_size("ta") * lax.axis_size("xyz")
    copies = jnp.broadcast_to(x[None], (count,) + x.shape)
    return jnp.sum(lax.all_to_all(copies, axes, 0, 0), axis=0)


def neighbour_source(device, stride, extent, step):
    coord = device // stride % extent
    return device + ((coord + step) % extent - coord) * stride


def both_sides(lowered, which, axis, stride, extent):
    length = lowered.shape[which]
    count = lax.axis_size(axis)
    first = lax.slice_in_dim(lowered, 0, 1, axis=which)
    last = lax.slice_in_dim(lowered, length - 1, length, axis=which)
    if extent == 1:
        from_upper, from_lower = first, last
    elif extent == 2:
        perm = [(neighbour_source(d, stride, extent, 1), d) for d in range(count)]
        if length == 1:
            from_upper = from_lower = lax.ppermute(first, axis, perm)
        else:
            pair = lax.ppermute(jnp.concatenate([first, last], which), axis, perm)
            from_upper = lax.slice_in_dim(pair, 0, 1, axis=which)
            from_lower = lax.slice_in_dim(pair, 1, 2, axis=which)
    else:
        up = [(neighbour_source(d, stride, extent, 1), d) for d in range(count)]
        down = [(neighbour_source(d, stride, extent, -1), d) for d in range(count)]
        from_upper = lax.ppermute(first, axis, up)
        from_lower = lax.ppermute(last, axis, down)
    upper = jnp.concatenate([lax.slice_in_dim(lowered, 1, length, axis=which), from_upper], which)
    lower = jnp.concatenate(
        [from_lower, lax.slice_in_dim(lowered, 0, length - 1, axis=which)], which
    )
    return (upper, lower)


def apply_links(coarse_links, lowered):
    blocks_total = lax.axis_size("xyz")
    across_x = 2 + 2 * min(blocks_total // 64, 1)
    across_z = blocks_total // (across_x * across_x)
    upper_x, lower_x = both_sides(lowered, 5, "xyz", 1, across_x)
    upper_y, lower_y = both_sides(lowered, 4, "xyz", across_x, across_x)
    upper_z, lower_z = both_sides(lowered, 3, "xyz", across_x * across_x, across_z)
    upper_t, lower_t = both_sides(lowered, 1, "ta", 1, lax.axis_size("ta"))
    stacked = jnp.stack(
        [lowered, upper_x, lower_x, upper_y, lower_y, upper_z, lower_z, upper_t, lower_t], 2
    )
    half_width = lowered.shape[-1] // 2
    real_part = stacked[..., :half_width]
    imag_part = stacked[..., half_width:]
    real_input = jnp.concatenate([real_part, -imag_part], -1)
    imag_input = jnp.concatenate([imag_part, real_part], -1)
    inputs = jnp.stack([real_input, imag_input], 0)
    result = jnp.einsum(
        "tbzyxdik,pntdbzyxk->pntbzyxi", coarse_links, inputs, preferred_element_type=jnp.float32
    )
    return jnp.concatenate([result[0], result[1]], -1)


def restrict_exact(null_vectors, field):
    return jnp.einsum(
        "tbzyxjk,ntbzyxk->nj",
        null_vectors.astype(jnp.float32),
        field,
        preferred_element_type=jnp.float32,
        precision=lax.Precision.HIGH,
    )


def slab_columns(parts):
    return jnp.transpose(parts, (1, 0, 2)).reshape(parts.shape[1], -1)


def finish(vector_in, slab, null_vectors, inverse_rows):
    correction = lax.dot_general(
        slab,
        inverse_rows,
        (((1,), (1,)), ((), ())),
        preferred_element_type=jnp.float32,
    ).astype(jnp.bfloat16)
    prolonged = jnp.einsum(
        "tbzyxjk,nj->ntbzyxk", null_vectors, correction, preferred_element_type=jnp.float32
    )
    return OMEGA * vector_in + prolonged


def inner_rows(left_vec, right_vec):
    return jnp.sum(left_vec * right_vec, axis=(1, 2, 3, 4, 5, 6))


def scaled(weights, vector_in):
    return weights[:, None, None, None, None, None, None] * vector_in


def shards(right_side, coarse_links, null_vectors, coarse_inverse):
    inverse_rows = coarse_inverse[0]
    slabs_total = lax.axis_size("ta")
    blocks_total = lax.axis_size("xyz")
    residual = right_side
    coarse = jnp.einsum(
        "tbzyxjk,ntbzyxk->nj",
        null_vectors,
        residual.astype(jnp.bfloat16),
        preferred_element_type=jnp.float32,
    ).astype(jnp.bfloat16)
    parts = lax.all_to_all(
        jnp.broadcast_to(coarse[None], (blocks_total,) + coarse.shape), "xyz", 0, 0
    )
    slab_a = slab_columns(parts)
    direction_a = finish(residual, slab_a, null_vectors, inverse_rows)
    image_a = apply_links(coarse_links, direction_a.astype(jnp.bfloat16))
    image_coarse = jnp.concatenate(
        [restrict_exact(null_vectors, residual), restrict_exact(null_vectors, image_a)], 1
    )
    width = image_coarse.shape[1] // 2
    pair_local = jnp.stack([inner_rows(image_a, image_a), inner_rows(image_a, residual)], 1)
    if slabs_total * blocks_total <= 64:
        local = jnp.concatenate([pair_local, image_coarse], 1)
        gathered = lax.all_to_all(
            jnp.broadcast_to(local[None], (slabs_total * blocks_total,) + local.shape),
            ("ta", "xyz"),
            0,
            0,
        )
        pair = jnp.sum(gathered[:, :, :2], axis=0)
        slabs = lax.dynamic_index_in_dim(
            gathered[:, :, 2:].reshape((slabs_total, blocks_total) + image_coarse.shape),
            lax.axis_index("ta"),
            0,
            keepdims=False,
        )
    else:
        pair = total_sum(pair_local)
        slabs = lax.all_to_all(
            jnp.broadcast_to(image_coarse[None], (blocks_total,) + image_coarse.shape),
            "xyz",
            0,
            0,
        )
    slab_residual = slab_columns(slabs[:, :, :width])
    slab_image = slab_columns(slabs[:, :, width:])
    norm_a, correlation_a = pair[:, 0], pair[:, 1]
    step_a = correlation_a / (norm_a + EPS)
    solution = scaled(step_a, direction_a)
    residual = residual - scaled(step_a, image_a)
    slab_b = (slab_residual - step_a[:, None] * slab_image).astype(jnp.bfloat16)
    direction_b = finish(residual, slab_b, null_vectors, inverse_rows)
    image_b = apply_links(coarse_links, direction_b.astype(jnp.bfloat16))
    sums = total_sum(
        jnp.stack(
            [
                inner_rows(image_a, image_b),
                inner_rows(image_b, image_b),
                inner_rows(image_b, residual),
                inner_rows(image_a, residual),
            ]
        )
    )
    projection_sum, square_b, raw_correlation, shared_correlation = (
        sums[0], sums[1], sums[2], sums[3]
    )
    beta_coef = projection_sum / (norm_a + EPS)
    image_b = image_b - scaled(beta_coef, image_a)
    direction_b = direction_b - scaled(beta_coef, direction_a)
    norm_b = jnp.maximum(
        square_b - beta_coef * (2.0 * projection_sum - beta_coef * norm_a), 0.0
    )
    correlation_b = raw_correlation - beta_coef * shared_correlation
    step_b = correlation_b / (norm_b + EPS)
    solution = solution + scaled(step_b, direction_b)
    residual = residual - scaled(step_b, image_b)
    return (solution, residual)


def solution(mesh):
    in_specs = (
        P(None, "ta", "xyz", None, None, None, None),
        P("ta", "xyz", None, None, None, None, None, None),
        P("ta", "xyz", None, None, None, None, None),
        P("ta", "xyz", None),
    )
    out_specs = (
        P(None, "ta", "xyz", None, None, None, None),
        P(None, "ta", "xyz", None, None, None, None),
    )
    return jax.shard_map(shards, mesh=mesh, in_specs=in_specs, out_specs=out_specs, check_vma=False)
```

```python
import jax
import jax.numpy as jnp
from jax import lax
from jax.sharding import PartitionSpec as P

OMEGA = 0.4
EPS = 1e-06


def is_power_of_two(count):
    return count & (count - 1) == 0


def exchange(x, axis, bit):
    count = lax.axis_size(axis)
    return lax.ppermute(x, axis, [(i, i ^ bit) for i in range(count)])


def axis_sum(x, axis):
    count = lax.axis_size(axis)
    if not is_power_of_two(count):
        return lax.psum(x, axis)
    bit = 1
    while bit < count:
        x = x + exchange(x, axis, bit)
        bit *= 2
    return x


def total_sum(x):
    axes = ("ta", "xyz")
    count = lax.axis_size("ta") * lax.axis_size("xyz")
    copies = jnp.broadcast_to(x[None], (count,) + x.shape)
    return jnp.sum(lax.all_to_all(copies, axes, 0, 0), axis=0)


def neighbour_source(device, stride, extent, step):
    coord = device // stride % extent
    return device + ((coord + step) % extent - coord) * stride


def both_sides(lowered, which, axis, stride, extent):
    length = lowered.shape[which]
    count = lax.axis_size(axis)
    first = lax.slice_in_dim(lowered, 0, 1, axis=which)
    last = lax.slice_in_dim(lowered, length - 1, length, axis=which)
    if extent == 1:
        from_upper, from_lower = first, last
    elif extent == 2:
        perm = [(neighbour_source(d, stride, extent, 1), d) for d in range(count)]
        if length == 1:
            from_upper = from_lower = lax.ppermute(first, axis, perm)
        else:
            pair = lax.ppermute(jnp.concatenate([first, last], which), axis, perm)
            from_upper = lax.slice_in_dim(pair, 0, 1, axis=which)
            from_lower = lax.slice_in_dim(pair, 1, 2, axis=which)
    else:
        up = [(neighbour_source(d, stride, extent, 1), d) for d in range(count)]
        down = [(neighbour_source(d, stride, extent, -1), d) for d in range(count)]
        from_upper = lax.ppermute(first, axis, up)
        from_lower = lax.ppermute(last, axis, down)
    upper = jnp.concatenate([lax.slice_in_dim(lowered, 1, length, axis=which), from_upper], which)
    lower = jnp.concatenate(
        [from_lower, lax.slice_in_dim(lowered, 0, length - 1, axis=which)], which
    )
    return (upper, lower)


def apply_links(coarse_links, lowered):
    blocks_total = lax.axis_size("xyz")
    across_x = 2 + 2 * min(blocks_total // 64, 1)
    across_z = blocks_total // (across_x * across_x)
    upper_x, lower_x = both_sides(lowered, 5, "xyz", 1, across_x)
    upper_y, lower_y = both_sides(lowered, 4, "xyz", across_x, across_x)
    upper_z, lower_z = both_sides(lowered, 3, "xyz", across_x * across_x, across_z)
    upper_t, lower_t = both_sides(lowered, 1, "ta", 1, lax.axis_size("ta"))
    stacked = jnp.stack(
        [lowered, upper_x, lower_x, upper_y, lower_y, upper_z, lower_z, upper_t, lower_t], 2
    )
    half_width = lowered.shape[-1] // 2
    real_part = stacked[..., :half_width]
    imag_part = stacked[..., half_width:]
    real_input = jnp.concatenate([real_part, -imag_part], -1)
    imag_input = jnp.concatenate([imag_part, real_part], -1)
    inputs = jnp.stack([real_input, imag_input], 0)
    result = jnp.einsum(
        "tbzyxdik,pntdbzyxk->pntbzyxi", coarse_links, inputs, preferred_element_type=jnp.float32
    )
    return jnp.concatenate([result[0], result[1]], -1)


def restrict_exact(null_vectors, field):
    return jnp.einsum(
        "tbzyxjk,ntbzyxk->nj",
        null_vectors.astype(jnp.float32),
        field,
        preferred_element_type=jnp.float32,
        precision=lax.Precision.HIGHEST,
    )


def slab_columns(parts):
    return jnp.transpose(parts, (1, 0, 2)).reshape(parts.shape[1], -1)


def finish(vector_in, slab, null_vectors, inverse_rows):
    correction = lax.dot_general(
        slab,
        inverse_rows,
        (((1,), (1,)), ((), ())),
        preferred_element_type=jnp.float32,
    ).astype(jnp.bfloat16)
    prolonged = jnp.einsum(
        "tbzyxjk,nj->ntbzyxk", null_vectors, correction, preferred_element_type=jnp.float32
    )
    return OMEGA * vector_in + prolonged


def inner_rows(left_vec, right_vec):
    return jnp.sum(left_vec * right_vec, axis=(1, 2, 3, 4, 5, 6))


def scaled(weights, vector_in):
    return weights[:, None, None, None, None, None, None] * vector_in


def shards(right_side, coarse_links, null_vectors, coarse_inverse):
    inverse_rows = coarse_inverse[0]
    slabs_total = lax.axis_size("ta")
    blocks_total = lax.axis_size("xyz")
    residual = right_side
    coarse = jnp.einsum(
        "tbzyxjk,ntbzyxk->nj",
        null_vectors,
        residual.astype(jnp.bfloat16),
        preferred_element_type=jnp.float32,
    ).astype(jnp.bfloat16)
    width = coarse.shape[1]
    payload = jnp.concatenate(
        [coarse.astype(jnp.float32), restrict_exact(null_vectors, residual)], 1
    )
    parts = lax.all_to_all(
        jnp.broadcast_to(payload[None], (blocks_total,) + payload.shape), "xyz", 0, 0
    )
    slab_a = slab_columns(parts[:, :, :width]).astype(jnp.bfloat16)
    slab_residual = slab_columns(parts[:, :, width:])
    direction_a = finish(residual, slab_a, null_vectors, inverse_rows)
    image_a = apply_links(coarse_links, direction_a.astype(jnp.bfloat16))
    image_coarse = restrict_exact(null_vectors, image_a)
    pair_local = jnp.stack([inner_rows(image_a, image_a), inner_rows(image_a, residual)], 1)
    if slabs_total * blocks_total <= 64:
        devices = slabs_total * blocks_total
        count, width = image_coarse.shape
        local = jnp.concatenate([pair_local.T.reshape(-1), image_coarse.reshape(-1)])
        gathered = lax.all_to_all(
            jnp.broadcast_to(local[None, None], (devices, 1) + local.shape),
            ("ta", "xyz"),
            0,
            0,
        )[:, 0]
        pair = jnp.sum(gathered[:, : 2 * count], axis=0).reshape(2, count).T
        image_slabs = gathered[:, 2 * count :].reshape(
            (slabs_total, blocks_total, count, width)
        )
        slab_image = slab_columns(
            lax.dynamic_index_in_dim(image_slabs, lax.axis_index("ta"), 0, keepdims=False)
        )
    else:
        pair = total_sum(pair_local)
        slab_image = slab_columns(
            lax.all_to_all(
                jnp.broadcast_to(image_coarse[None], (blocks_total,) + image_coarse.shape),
                "xyz",
                0,
                0,
            )
        )
    norm_a, correlation_a = pair[:, 0], pair[:, 1]
    step_a = correlation_a / (norm_a + EPS)
    solution = scaled(step_a, direction_a)
    residual = residual - scaled(step_a, image_a)
    slab_b = (slab_residual - step_a[:, None] * slab_image).astype(jnp.bfloat16)
    direction_b = finish(residual, slab_b, null_vectors, inverse_rows)
    image_b = apply_links(coarse_links, direction_b.astype(jnp.bfloat16))
    sums = total_sum(
        jnp.stack(
            [
                inner_rows(image_a, image_b),
                inner_rows(image_b, image_b),
                inner_rows(image_b, residual),
                inner_rows(image_a, residual),
            ]
        )
    )
    projection_sum, square_b, raw_correlation, shared_correlation = (
        sums[0], sums[1], sums[2], sums[3]
    )
    beta_coef = projection_sum / (norm_a + EPS)
    image_b = image_b - scaled(beta_coef, image_a)
    direction_b = direction_b - scaled(beta_coef, direction_a)
    norm_b = jnp.maximum(
        square_b - beta_coef * (2.0 * projection_sum - beta_coef * norm_a), 0.0
    )
    correlation_b = raw_correlation - beta_coef * shared_correlation
    step_b = correlation_b / (norm_b + EPS)
    solution = solution + scaled(step_b, direction_b)
    residual = residual - scaled(step_b, image_b)
    return (solution, residual)


def solution(mesh):
    in_specs = (
        P(None, "ta", "xyz", None, None, None, None),
        P("ta", "xyz", None, None, None, None, None, None),
        P("ta", "xyz", None, None, None, None, None),
        P("ta", "xyz", None),
    )
    out_specs = (
        P(None, "ta", "xyz", None, None, None, None),
        P(None, "ta", "xyz", None, None, None, None),
    )
    return jax.shard_map(shards, mesh=mesh, in_specs=in_specs, out_specs=out_specs, check_vma=False)
```

```python
import jax
import jax.numpy as jnp
from jax import lax
from jax.sharding import PartitionSpec as P

OMEGA = 0.4
EPS = 1e-06


def is_power_of_two(count):
    return count & (count - 1) == 0


def exchange(x, axis, bit):
    count = lax.axis_size(axis)
    return lax.ppermute(x, axis, [(i, i ^ bit) for i in range(count)])


def axis_sum(x, axis):
    count = lax.axis_size(axis)
    if not is_power_of_two(count):
        return lax.psum(x, axis)
    bit = 1
    while bit < count:
        x = x + exchange(x, axis, bit)
        bit *= 2
    return x


def total_sum(x):
    axes = ("ta", "xyz")
    count = lax.axis_size("ta") * lax.axis_size("xyz")
    flat = x.reshape(-1)
    copies = jnp.broadcast_to(flat[None, None], (count, 1) + flat.shape)
    return jnp.sum(lax.all_to_all(copies, axes, 0, 0)[:, 0], axis=0).reshape(x.shape)


def neighbour_source(device, stride, extent, step):
    coord = device // stride % extent
    return device + ((coord + step) % extent - coord) * stride


def both_sides(lowered, which, axis, stride, extent):
    length = lowered.shape[which]
    count = lax.axis_size(axis)
    first = lax.slice_in_dim(lowered, 0, 1, axis=which)
    last = lax.slice_in_dim(lowered, length - 1, length, axis=which)
    if extent == 1:
        from_upper, from_lower = first, last
    elif extent == 2:
        perm = [(neighbour_source(d, stride, extent, 1), d) for d in range(count)]
        if length == 1:
            from_upper = from_lower = lax.ppermute(first, axis, perm)
        else:
            pair = lax.ppermute(jnp.concatenate([first, last], which), axis, perm)
            from_upper = lax.slice_in_dim(pair, 0, 1, axis=which)
            from_lower = lax.slice_in_dim(pair, 1, 2, axis=which)
    else:
        up = [(neighbour_source(d, stride, extent, 1), d) for d in range(count)]
        down = [(neighbour_source(d, stride, extent, -1), d) for d in range(count)]
        from_upper = lax.ppermute(first, axis, up)
        from_lower = lax.ppermute(last, axis, down)
    upper = jnp.concatenate([lax.slice_in_dim(lowered, 1, length, axis=which), from_upper], which)
    lower = jnp.concatenate(
        [from_lower, lax.slice_in_dim(lowered, 0, length - 1, axis=which)], which
    )
    return (upper, lower)


def apply_links(coarse_links, lowered):
    blocks_total = lax.axis_size("xyz")
    across_x = 2 + 2 * min(blocks_total // 64, 1)
    across_z = blocks_total // (across_x * across_x)
    upper_x, lower_x = both_sides(lowered, 5, "xyz", 1, across_x)
    upper_y, lower_y = both_sides(lowered, 4, "xyz", across_x, across_x)
    upper_z, lower_z = both_sides(lowered, 3, "xyz", across_x * across_x, across_z)
    upper_t, lower_t = both_sides(lowered, 1, "ta", 1, lax.axis_size("ta"))
    stacked = jnp.stack(
        [lowered, upper_x, lower_x, upper_y, lower_y, upper_z, lower_z, upper_t, lower_t], 2
    )
    half_width = lowered.shape[-1] // 2
    real_part = stacked[..., :half_width]
    imag_part = stacked[..., half_width:]
    real_input = jnp.concatenate([real_part, -imag_part], -1)
    imag_input = jnp.concatenate([imag_part, real_part], -1)
    inputs = jnp.stack([real_input, imag_input], 0)
    result = jnp.einsum(
        "tbzyxdik,pntdbzyxk->pntbzyxi", coarse_links, inputs, preferred_element_type=jnp.float32
    )
    return jnp.concatenate([result[0], result[1]], -1)


def restrict_exact(null_vectors, field):
    return jnp.einsum(
        "tbzyxjk,ntbzyxk->nj",
        null_vectors.astype(jnp.float32),
        field,
        preferred_element_type=jnp.float32,
        precision=lax.Precision.HIGH,
    )


def slab_columns(parts):
    return jnp.transpose(parts, (1, 0, 2)).reshape(parts.shape[1], -1)


def finish(vector_in, slab, null_vectors, inverse_rows):
    correction = lax.dot_general(
        slab,
        inverse_rows,
        (((1,), (1,)), ((), ())),
        preferred_element_type=jnp.float32,
    ).astype(jnp.bfloat16)
    prolonged = jnp.einsum(
        "tbzyxjk,nj->ntbzyxk", null_vectors, correction, preferred_element_type=jnp.float32
    )
    return OMEGA * vector_in + prolonged


def inner_rows(left_vec, right_vec):
    return jnp.sum(left_vec * right_vec, axis=(1, 2, 3, 4, 5, 6))


def scaled(weights, vector_in):
    return weights[:, None, None, None, None, None, None] * vector_in


def shards(right_side, coarse_links, null_vectors, coarse_inverse):
    inverse_rows = coarse_inverse[0]
    slabs_total = lax.axis_size("ta")
    blocks_total = lax.axis_size("xyz")
    residual = right_side
    coarse = jnp.einsum(
        "tbzyxjk,ntbzyxk->nj",
        null_vectors,
        residual.astype(jnp.bfloat16),
        preferred_element_type=jnp.float32,
    ).astype(jnp.bfloat16)
    width = coarse.shape[1]
    payload = jnp.concatenate(
        [coarse.astype(jnp.float32), restrict_exact(null_vectors, residual)], 1
    )
    parts = lax.all_to_all(
        jnp.broadcast_to(payload[None], (blocks_total,) + payload.shape), "xyz", 0, 0
    )
    slab_a = slab_columns(parts[:, :, :width]).astype(jnp.bfloat16)
    slab_residual = slab_columns(parts[:, :, width:])
    direction_a = finish(residual, slab_a, null_vectors, inverse_rows)
    image_a = apply_links(coarse_links, direction_a.astype(jnp.bfloat16))
    image_coarse = restrict_exact(null_vectors, image_a)
    pair_local = jnp.stack([inner_rows(image_a, image_a), inner_rows(image_a, residual)], 1)
    if slabs_total * blocks_total <= 64:
        devices = slabs_total * blocks_total
        count, width = image_coarse.shape
        local = jnp.concatenate([pair_local.T.reshape(-1), image_coarse.reshape(-1)])
        gathered = lax.all_to_all(
            jnp.broadcast_to(local[None, None], (devices, 1) + local.shape),
            ("ta", "xyz"),
            0,
            0,
        )[:, 0]
        pair = jnp.sum(gathered[:, : 2 * count], axis=0).reshape(2, count).T
        image_slabs = gathered[:, 2 * count :].reshape(
            (slabs_total, blocks_total, count, width)
        )
        slab_image = slab_columns(
            lax.dynamic_index_in_dim(image_slabs, lax.axis_index("ta"), 0, keepdims=False)
        )
    else:
        pair = total_sum(pair_local)
        slab_image = slab_columns(
            lax.all_to_all(
                jnp.broadcast_to(image_coarse[None], (blocks_total,) + image_coarse.shape),
                "xyz",
                0,
                0,
            )
        )
    norm_a, correlation_a = pair[:, 0], pair[:, 1]
    step_a = correlation_a / (norm_a + EPS)
    solution = scaled(step_a, direction_a)
    residual = residual - scaled(step_a, image_a)
    slab_b = (slab_residual - step_a[:, None] * slab_image).astype(jnp.bfloat16)
    direction_b = finish(residual, slab_b, null_vectors, inverse_rows)
    image_b = apply_links(coarse_links, direction_b.astype(jnp.bfloat16))
    sums = total_sum(
        jnp.stack(
            [
                inner_rows(image_a, image_b),
                inner_rows(image_b, image_b),
                inner_rows(image_b, residual),
                inner_rows(image_a, residual),
            ]
        )
    )
    projection_sum, square_b, raw_correlation, shared_correlation = (
        sums[0], sums[1], sums[2], sums[3]
    )
    beta_coef = projection_sum / (norm_a + EPS)
    image_b = image_b - scaled(beta_coef, image_a)
    direction_b = direction_b - scaled(beta_coef, direction_a)
    norm_b = jnp.maximum(
        square_b - beta_coef * (2.0 * projection_sum - beta_coef * norm_a), 0.0
    )
    correlation_b = raw_correlation - beta_coef * shared_correlation
    step_b = correlation_b / (norm_b + EPS)
    solution = solution + scaled(step_b, direction_b)
    residual = residual - scaled(step_b, image_b)
    return (solution, residual)


def solution(mesh):
    in_specs = (
        P(None, "ta", "xyz", None, None, None, None),
        P("ta", "xyz", None, None, None, None, None, None),
        P("ta", "xyz", None, None, None, None, None),
        P("ta", "xyz", None),
    )
    out_specs = (
        P(None, "ta", "xyz", None, None, None, None),
        P(None, "ta", "xyz", None, None, None, None),
    )
    return jax.shard_map(shards, mesh=mesh, in_specs=in_specs, out_specs=out_specs, check_vma=False)
```

```python
import jax
import jax.numpy as jnp
from jax import lax
from jax.sharding import PartitionSpec as P

OMEGA = 0.4
EPS = 1e-06


def is_power_of_two(count):
    return count & (count - 1) == 0


def exchange(x, axis, bit):
    count = lax.axis_size(axis)
    return lax.ppermute(x, axis, [(i, i ^ bit) for i in range(count)])


def axis_sum(x, axis):
    count = lax.axis_size(axis)
    if not is_power_of_two(count):
        return lax.psum(x, axis)
    bit = 1
    while bit < count:
        x = x + exchange(x, axis, bit)
        bit *= 2
    return x


def total_sum(x):
    axes = ("ta", "xyz")
    count = lax.axis_size("ta") * lax.axis_size("xyz")
    flat = x.reshape(-1)
    copies = jnp.broadcast_to(flat[None, None], (count, 1) + flat.shape)
    return jnp.sum(lax.all_to_all(copies, axes, 0, 0)[:, 0], axis=0).reshape(x.shape)


def neighbour_source(device, stride, extent, step):
    coord = device // stride % extent
    return device + ((coord + step) % extent - coord) * stride


def both_sides(lowered, which, axis, stride, extent):
    length = lowered.shape[which]
    count = lax.axis_size(axis)
    first = lax.slice_in_dim(lowered, 0, 1, axis=which)
    last = lax.slice_in_dim(lowered, length - 1, length, axis=which)
    if extent == 1:
        from_upper, from_lower = first, last
    elif extent == 2:
        perm = [(neighbour_source(d, stride, extent, 1), d) for d in range(count)]
        if length == 1:
            from_upper = from_lower = lax.ppermute(first, axis, perm)
        else:
            pair = lax.ppermute(jnp.concatenate([first, last], which), axis, perm)
            from_upper = lax.slice_in_dim(pair, 0, 1, axis=which)
            from_lower = lax.slice_in_dim(pair, 1, 2, axis=which)
    else:
        up = [(neighbour_source(d, stride, extent, 1), d) for d in range(count)]
        down = [(neighbour_source(d, stride, extent, -1), d) for d in range(count)]
        from_upper = lax.ppermute(first, axis, up)
        from_lower = lax.ppermute(last, axis, down)
    upper = jnp.concatenate([lax.slice_in_dim(lowered, 1, length, axis=which), from_upper], which)
    lower = jnp.concatenate(
        [from_lower, lax.slice_in_dim(lowered, 0, length - 1, axis=which)], which
    )
    return (upper, lower)


def apply_links(coarse_links, lowered):
    blocks_total = lax.axis_size("xyz")
    across_x = 2 + 2 * min(blocks_total // 64, 1)
    across_z = blocks_total // (across_x * across_x)
    upper_x, lower_x = both_sides(lowered, 5, "xyz", 1, across_x)
    upper_y, lower_y = both_sides(lowered, 4, "xyz", across_x, across_x)
    upper_z, lower_z = both_sides(lowered, 3, "xyz", across_x * across_x, across_z)
    upper_t, lower_t = both_sides(lowered, 1, "ta", 1, lax.axis_size("ta"))
    stacked = jnp.stack(
        [lowered, upper_x, lower_x, upper_y, lower_y, upper_z, lower_z, upper_t, lower_t], 2
    )
    half_width = lowered.shape[-1] // 2
    real_part = stacked[..., :half_width]
    imag_part = stacked[..., half_width:]
    real_input = jnp.concatenate([real_part, -imag_part], -1)
    imag_input = jnp.concatenate([imag_part, real_part], -1)
    inputs = jnp.stack([real_input, imag_input], 0)
    result = jnp.einsum(
        "tbzyxdik,pntdbzyxk->pntbzyxi", coarse_links, inputs, preferred_element_type=jnp.float32
    )
    return jnp.concatenate([result[0], result[1]], -1)


def restrict_exact(null_vectors, field):
    return jnp.einsum(
        "tbzyxjk,ntbzyxk->nj",
        null_vectors.astype(jnp.float32),
        field,
        preferred_element_type=jnp.float32,
        precision=lax.Precision.HIGH,
    )


def slab_columns(parts):
    return jnp.transpose(parts, (1, 0, 2)).reshape(parts.shape[1], -1)


def finish(vector_in, slab, null_vectors, inverse_rows):
    correction = lax.dot_general(
        slab,
        inverse_rows,
        (((1,), (1,)), ((), ())),
        preferred_element_type=jnp.float32,
    ).astype(jnp.bfloat16)
    prolonged = jnp.einsum(
        "tbzyxjk,nj->ntbzyxk", null_vectors, correction, preferred_element_type=jnp.float32
    )
    return OMEGA * vector_in + prolonged


def inner_rows(left_vec, right_vec):
    return jnp.sum(left_vec * right_vec, axis=(1, 2, 3, 4, 5, 6))


def scaled(weights, vector_in):
    return weights[:, None, None, None, None, None, None] * vector_in


def shards(right_side, coarse_links, null_vectors, coarse_inverse):
    inverse_rows = coarse_inverse[0]
    slabs_total = lax.axis_size("ta")
    blocks_total = lax.axis_size("xyz")
    residual = right_side
    exact_residual = restrict_exact(null_vectors, residual)
    parts = lax.all_to_all(
        jnp.broadcast_to(exact_residual[None], (blocks_total,) + exact_residual.shape),
        "xyz",
        0,
        0,
    )
    slab_residual = slab_columns(parts)
    slab_a = slab_residual.astype(jnp.bfloat16)
    direction_a = finish(residual, slab_a, null_vectors, inverse_rows)
    image_a = apply_links(coarse_links, direction_a.astype(jnp.bfloat16))
    image_coarse = restrict_exact(null_vectors, image_a)
    pair_local = jnp.stack([inner_rows(image_a, image_a), inner_rows(image_a, residual)], 1)
    if slabs_total * blocks_total <= 64:
        devices = slabs_total * blocks_total
        count, width = image_coarse.shape
        local = jnp.concatenate([pair_local.T.reshape(-1), image_coarse.reshape(-1)])
        gathered = lax.all_to_all(
            jnp.broadcast_to(local[None, None], (devices, 1) + local.shape),
            ("ta", "xyz"),
            0,
            0,
        )[:, 0]
        pair = jnp.sum(gathered[:, : 2 * count], axis=0).reshape(2, count).T
        image_slabs = gathered[:, 2 * count :].reshape(
            (slabs_total, blocks_total, count, width)
        )
        slab_image = slab_columns(
            lax.dynamic_index_in_dim(image_slabs, lax.axis_index("ta"), 0, keepdims=False)
        )
    else:
        pair = total_sum(pair_local)
        slab_image = slab_columns(
            lax.all_to_all(
                jnp.broadcast_to(image_coarse[None], (blocks_total,) + image_coarse.shape),
                "xyz",
                0,
                0,
            )
        )
    norm_a, correlation_a = pair[:, 0], pair[:, 1]
    step_a = correlation_a / (norm_a + EPS)
    solution = scaled(step_a, direction_a)
    residual = residual - scaled(step_a, image_a)
    slab_b = (slab_residual - step_a[:, None] * slab_image).astype(jnp.bfloat16)
    direction_b = finish(residual, slab_b, null_vectors, inverse_rows)
    image_b = apply_links(coarse_links, direction_b.astype(jnp.bfloat16))
    sums = total_sum(
        jnp.stack(
            [
                inner_rows(image_a, image_b),
                inner_rows(image_b, image_b),
                inner_rows(image_b, residual),
                inner_rows(image_a, residual),
            ]
        )
    )
    projection_sum, square_b, raw_correlation, shared_correlation = (
        sums[0], sums[1], sums[2], sums[3]
    )
    beta_coef = projection_sum / (norm_a + EPS)
    image_b = image_b - scaled(beta_coef, image_a)
    direction_b = direction_b - scaled(beta_coef, direction_a)
    norm_b = jnp.maximum(
        square_b - beta_coef * (2.0 * projection_sum - beta_coef * norm_a), 0.0
    )
    correlation_b = raw_correlation - beta_coef * shared_correlation
    step_b = correlation_b / (norm_b + EPS)
    solution = solution + scaled(step_b, direction_b)
    residual = residual - scaled(step_b, image_b)
    return (solution, residual)


def solution(mesh):
    in_specs = (
        P(None, "ta", "xyz", None, None, None, None),
        P("ta", "xyz", None, None, None, None, None, None),
        P("ta", "xyz", None, None, None, None, None),
        P("ta", "xyz", None),
    )
    out_specs = (
        P(None, "ta", "xyz", None, None, None, None),
        P(None, "ta", "xyz", None, None, None, None),
    )
    return jax.shard_map(shards, mesh=mesh, in_specs=in_specs, out_specs=out_specs, check_vma=False)
```

```python
import jax
import jax.numpy as jnp
from jax import lax
from jax.sharding import PartitionSpec as P

OMEGA = 0.4
EPS = 1e-06


def is_power_of_two(count):
    return count & (count - 1) == 0


def exchange(x, axis, bit):
    count = lax.axis_size(axis)
    return lax.ppermute(x, axis, [(i, i ^ bit) for i in range(count)])


def axis_sum(x, axis):
    count = lax.axis_size(axis)
    if not is_power_of_two(count):
        return lax.psum(x, axis)
    bit = 1
    while bit < count:
        x = x + exchange(x, axis, bit)
        bit *= 2
    return x


def total_sum(x):
    axes = ("ta", "xyz")
    count = lax.axis_size("ta") * lax.axis_size("xyz")
    flat = x.reshape(-1)
    copies = jnp.broadcast_to(flat[None, None], (count, 1) + flat.shape)
    return jnp.sum(lax.all_to_all(copies, axes, 0, 0)[:, 0], axis=0).reshape(x.shape)


def neighbour_source(device, stride, extent, step):
    coord = device // stride % extent
    return device + ((coord + step) % extent - coord) * stride


def both_sides(lowered, which, axis, stride, extent):
    length = lowered.shape[which]
    count = lax.axis_size(axis)
    first = lax.slice_in_dim(lowered, 0, 1, axis=which)
    last = lax.slice_in_dim(lowered, length - 1, length, axis=which)
    if extent == 1:
        from_upper, from_lower = first, last
    elif extent == 2:
        perm = [(neighbour_source(d, stride, extent, 1), d) for d in range(count)]
        if length == 1:
            from_upper = from_lower = lax.ppermute(first, axis, perm)
        else:
            pair = lax.ppermute(jnp.concatenate([first, last], which), axis, perm)
            from_upper = lax.slice_in_dim(pair, 0, 1, axis=which)
            from_lower = lax.slice_in_dim(pair, 1, 2, axis=which)
    else:
        up = [(neighbour_source(d, stride, extent, 1), d) for d in range(count)]
        down = [(neighbour_source(d, stride, extent, -1), d) for d in range(count)]
        from_upper = lax.ppermute(first, axis, up)
        from_lower = lax.ppermute(last, axis, down)
    upper = jnp.concatenate([lax.slice_in_dim(lowered, 1, length, axis=which), from_upper], which)
    lower = jnp.concatenate(
        [from_lower, lax.slice_in_dim(lowered, 0, length - 1, axis=which)], which
    )
    return (upper, lower)


def apply_links(coarse_links, lowered):
    blocks_total = lax.axis_size("xyz")
    across_x = 2 + 2 * min(blocks_total // 64, 1)
    across_z = blocks_total // (across_x * across_x)
    upper_x, lower_x = both_sides(lowered, 5, "xyz", 1, across_x)
    upper_y, lower_y = both_sides(lowered, 4, "xyz", across_x, across_x)
    upper_z, lower_z = both_sides(lowered, 3, "xyz", across_x * across_x, across_z)
    upper_t, lower_t = both_sides(lowered, 1, "ta", 1, lax.axis_size("ta"))
    stacked = jnp.stack(
        [lowered, upper_x, lower_x, upper_y, lower_y, upper_z, lower_z, upper_t, lower_t], 2
    )
    half_width = lowered.shape[-1] // 2
    real_part = stacked[..., :half_width]
    imag_part = stacked[..., half_width:]
    real_input = jnp.concatenate([real_part, -imag_part], -1)
    imag_input = jnp.concatenate([imag_part, real_part], -1)
    inputs = jnp.stack([real_input, imag_input], 0)
    result = jnp.einsum(
        "tbzyxdik,pntdbzyxk->pntbzyxi", coarse_links, inputs, preferred_element_type=jnp.float32
    )
    return jnp.concatenate([result[0], result[1]], -1)


def restrict_exact(null_vectors, field):
    return jnp.einsum(
        "tbzyxjk,ntbzyxk->nj",
        null_vectors.astype(jnp.float32),
        field,
        preferred_element_type=jnp.float32,
        precision=lax.Precision.HIGH,
    )


def slab_columns(parts):
    return jnp.transpose(parts, (1, 0, 2)).reshape(parts.shape[1], -1)


def finish(vector_in, slab, null_vectors, inverse_rows):
    correction = lax.dot_general(
        slab,
        inverse_rows,
        (((1,), (1,)), ((), ())),
        preferred_element_type=jnp.float32,
    ).astype(jnp.bfloat16)
    prolonged = jnp.einsum(
        "tbzyxjk,nj->ntbzyxk", null_vectors, correction, preferred_element_type=jnp.float32
    )
    return OMEGA * vector_in + prolonged


def inner_rows(left_vec, right_vec):
    return jnp.sum(left_vec * right_vec, axis=(1, 2, 3, 4, 5, 6))


def scaled(weights, vector_in):
    return weights[:, None, None, None, None, None, None] * vector_in


def shards(right_side, coarse_links, null_vectors, coarse_inverse):
    inverse_rows = coarse_inverse[0]
    slabs_total = lax.axis_size("ta")
    blocks_total = lax.axis_size("xyz")
    residual = right_side
    coarse = jnp.einsum(
        "tbzyxjk,ntbzyxk->nj",
        null_vectors,
        residual.astype(jnp.bfloat16),
        preferred_element_type=jnp.float32,
    ).astype(jnp.bfloat16)
    width = coarse.shape[1]
    payload = jnp.concatenate(
        [coarse.astype(jnp.float32), restrict_exact(null_vectors, residual)], 1
    )
    parts = lax.all_to_all(
        jnp.broadcast_to(payload[None], (blocks_total,) + payload.shape), "xyz", 0, 0
    )
    slab_a = slab_columns(parts[:, :, :width]).astype(jnp.bfloat16)
    slab_residual = parts[:, :, width:].reshape(blocks_total, -1)
    direction_a = finish(residual, slab_a, null_vectors, inverse_rows)
    image_a = apply_links(coarse_links, direction_a.astype(jnp.bfloat16))
    image_coarse = restrict_exact(null_vectors, image_a)
    pair_local = jnp.stack([inner_rows(image_a, image_a), inner_rows(image_a, residual)], 1)
    if slabs_total * blocks_total <= 64:
        devices = slabs_total * blocks_total
        count, width = image_coarse.shape
        local = jnp.concatenate([pair_local.T.reshape(-1), image_coarse.reshape(-1)])
        gathered = lax.all_to_all(
            jnp.broadcast_to(local[None, None], (devices, 1) + local.shape),
            ("ta", "xyz"),
            0,
            0,
        )[:, 0]
        pair = jnp.sum(gathered[:, : 2 * count], axis=0).reshape(2, count).T
        image_slabs = gathered[:, 2 * count :].reshape(
            (slabs_total, blocks_total, count * width)
        )
        slab_image = lax.dynamic_index_in_dim(
            image_slabs, lax.axis_index("ta"), 0, keepdims=False
        )
    else:
        pair = total_sum(pair_local)
        slab_image = lax.all_to_all(
            jnp.broadcast_to(image_coarse[None], (blocks_total,) + image_coarse.shape),
            "xyz",
            0,
            0,
        ).reshape(blocks_total, -1)
    norm_a, correlation_a = pair[:, 0], pair[:, 1]
    step_a = correlation_a / (norm_a + EPS)
    solution = scaled(step_a, direction_a)
    residual = residual - scaled(step_a, image_a)
    steps = jnp.repeat(step_a, slab_image.shape[1] // step_a.shape[0])
    slab_b = (slab_residual - steps[None, :] * slab_image).astype(jnp.bfloat16)
    slab_b = slab_columns(slab_b.reshape(blocks_total, step_a.shape[0], -1))
    direction_b = finish(residual, slab_b, null_vectors, inverse_rows)
    image_b = apply_links(coarse_links, direction_b.astype(jnp.bfloat16))
    sums = total_sum(
        jnp.stack(
            [
                inner_rows(image_a, image_b),
                inner_rows(image_b, image_b),
                inner_rows(image_b, residual),
                inner_rows(image_a, residual),
            ]
        )
    )
    projection_sum, square_b, raw_correlation, shared_correlation = (
        sums[0], sums[1], sums[2], sums[3]
    )
    beta_coef = projection_sum / (norm_a + EPS)
    image_b = image_b - scaled(beta_coef, image_a)
    direction_b = direction_b - scaled(beta_coef, direction_a)
    norm_b = jnp.maximum(
        square_b - beta_coef * (2.0 * projection_sum - beta_coef * norm_a), 0.0
    )
    correlation_b = raw_correlation - beta_coef * shared_correlation
    step_b = correlation_b / (norm_b + EPS)
    solution = solution + scaled(step_b, direction_b)
    residual = residual - scaled(step_b, image_b)
    return (solution, residual)


def solution(mesh):
    in_specs = (
        P(None, "ta", "xyz", None, None, None, None),
        P("ta", "xyz", None, None, None, None, None, None),
        P("ta", "xyz", None, None, None, None, None),
        P("ta", "xyz", None),
    )
    out_specs = (
        P(None, "ta", "xyz", None, None, None, None),
        P(None, "ta", "xyz", None, None, None, None),
    )
    return jax.shard_map(shards, mesh=mesh, in_specs=in_specs, out_specs=out_specs, check_vma=False)
```

```python
import jax
import jax.numpy as jnp
from jax import lax
from jax.sharding import PartitionSpec as P

OMEGA = 0.4
EPS = 1e-06


def is_power_of_two(count):
    return count & (count - 1) == 0


def exchange(x, axis, bit):
    count = lax.axis_size(axis)
    return lax.ppermute(x, axis, [(i, i ^ bit) for i in range(count)])


def axis_sum(x, axis):
    count = lax.axis_size(axis)
    if not is_power_of_two(count):
        return lax.psum(x, axis)
    bit = 1
    while bit < count:
        x = x + exchange(x, axis, bit)
        bit *= 2
    return x


def total_sum(x):
    axes = ("ta", "xyz")
    count = lax.axis_size("ta") * lax.axis_size("xyz")
    flat = x.reshape(-1)
    copies = jnp.broadcast_to(flat[None, None], (count, 1) + flat.shape)
    return jnp.sum(lax.all_to_all(copies, axes, 0, 0)[:, 0], axis=0).reshape(x.shape)


def neighbour_source(device, stride, extent, step):
    coord = device // stride % extent
    return device + ((coord + step) % extent - coord) * stride


def both_sides(lowered, which, axis, stride, extent):
    length = lowered.shape[which]
    count = lax.axis_size(axis)
    first = lax.slice_in_dim(lowered, 0, 1, axis=which)
    last = lax.slice_in_dim(lowered, length - 1, length, axis=which)
    if extent == 1:
        from_upper, from_lower = first, last
    elif extent == 2:
        perm = [(neighbour_source(d, stride, extent, 1), d) for d in range(count)]
        if length == 1:
            from_upper = from_lower = lax.ppermute(first, axis, perm)
        else:
            pair = lax.ppermute(jnp.concatenate([first, last], which), axis, perm)
            from_upper = lax.slice_in_dim(pair, 0, 1, axis=which)
            from_lower = lax.slice_in_dim(pair, 1, 2, axis=which)
    else:
        up = [(neighbour_source(d, stride, extent, 1), d) for d in range(count)]
        down = [(neighbour_source(d, stride, extent, -1), d) for d in range(count)]
        from_upper = lax.ppermute(first, axis, up)
        from_lower = lax.ppermute(last, axis, down)
    upper = jnp.concatenate([lax.slice_in_dim(lowered, 1, length, axis=which), from_upper], which)
    lower = jnp.concatenate(
        [from_lower, lax.slice_in_dim(lowered, 0, length - 1, axis=which)], which
    )
    return (upper, lower)


def apply_links(coarse_links, lowered):
    blocks_total = lax.axis_size("xyz")
    across_x = 2 + 2 * min(blocks_total // 64, 1)
    across_z = blocks_total // (across_x * across_x)
    upper_x, lower_x = both_sides(lowered, 5, "xyz", 1, across_x)
    upper_y, lower_y = both_sides(lowered, 4, "xyz", across_x, across_x)
    upper_z, lower_z = both_sides(lowered, 3, "xyz", across_x * across_x, across_z)
    upper_t, lower_t = both_sides(lowered, 1, "ta", 1, lax.axis_size("ta"))
    stacked = jnp.stack(
        [lowered, upper_x, lower_x, upper_y, lower_y, upper_z, lower_z, upper_t, lower_t], 2
    )
    half_width = lowered.shape[-1] // 2
    real_part = stacked[..., :half_width]
    imag_part = stacked[..., half_width:]
    real_input = jnp.concatenate([real_part, -imag_part], -1)
    imag_input = jnp.concatenate([imag_part, real_part], -1)
    inputs = jnp.stack([real_input, imag_input], 0)
    result = jnp.einsum(
        "tbzyxdik,pntdbzyxk->pntbzyxi", coarse_links, inputs, preferred_element_type=jnp.float32
    )
    return jnp.concatenate([result[0], result[1]], -1)


def restrict_exact(null_vectors, field):
    return jnp.einsum(
        "tbzyxjk,ntbzyxk->nj",
        null_vectors.astype(jnp.float32),
        field,
        preferred_element_type=jnp.float32,
        precision=lax.Precision.HIGH,
    )


def slab_columns(parts):
    return jnp.transpose(parts, (1, 0, 2)).reshape(parts.shape[1], -1)


def finish(vector_in, slab, null_vectors, inverse_rows):
    correction = lax.dot_general(
        slab,
        inverse_rows,
        (((1,), (1,)), ((), ())),
        preferred_element_type=jnp.float32,
    ).astype(jnp.bfloat16)
    prolonged = jnp.einsum(
        "tbzyxjk,nj->ntbzyxk", null_vectors, correction, preferred_element_type=jnp.float32
    )
    return OMEGA * vector_in + prolonged


def inner_rows(left_vec, right_vec):
    return jnp.sum(left_vec * right_vec, axis=(1, 2, 3, 4, 5, 6))


def scaled(weights, vector_in):
    return weights[:, None, None, None, None, None, None] * vector_in


def shards(right_side, coarse_links, null_vectors, coarse_inverse):
    inverse_rows = coarse_inverse[0]
    slabs_total = lax.axis_size("ta")
    blocks_total = lax.axis_size("xyz")
    residual = right_side
    coarse = jnp.einsum(
        "tbzyxjk,ntbzyxk->nj",
        null_vectors,
        residual.astype(jnp.bfloat16),
        preferred_element_type=jnp.float32,
    ).astype(jnp.bfloat16)
    parts = lax.all_to_all(
        jnp.broadcast_to(coarse[None], (blocks_total,) + coarse.shape), "xyz", 0, 0
    )
    slab_a = slab_columns(parts)
    exact_residual = restrict_exact(null_vectors, residual)
    slab_residual = lax.all_to_all(
        jnp.broadcast_to(exact_residual[None], (blocks_total,) + exact_residual.shape),
        "xyz",
        0,
        0,
    ).reshape(blocks_total, -1)
    direction_a = finish(residual, slab_a, null_vectors, inverse_rows)
    image_a = apply_links(coarse_links, direction_a.astype(jnp.bfloat16))
    image_coarse = restrict_exact(null_vectors, image_a)
    pair_local = jnp.stack([inner_rows(image_a, image_a), inner_rows(image_a, residual)], 1)
    if slabs_total * blocks_total <= 64:
        devices = slabs_total * blocks_total
        count, width = image_coarse.shape
        local = jnp.concatenate([pair_local.T.reshape(-1), image_coarse.reshape(-1)])
        gathered = lax.all_to_all(
            jnp.broadcast_to(local[None, None], (devices, 1) + local.shape),
            ("ta", "xyz"),
            0,
            0,
        )[:, 0]
        pair = jnp.sum(gathered[:, : 2 * count], axis=0).reshape(2, count).T
        image_slabs = gathered[:, 2 * count :].reshape(
            (slabs_total, blocks_total, count * width)
        )
        slab_image = lax.dynamic_index_in_dim(
            image_slabs, lax.axis_index("ta"), 0, keepdims=False
        )
    else:
        pair = total_sum(pair_local)
        slab_image = lax.all_to_all(
            jnp.broadcast_to(image_coarse[None], (blocks_total,) + image_coarse.shape),
            "xyz",
            0,
            0,
        ).reshape(blocks_total, -1)
    norm_a, correlation_a = pair[:, 0], pair[:, 1]
    step_a = correlation_a / (norm_a + EPS)
    solution = scaled(step_a, direction_a)
    residual = residual - scaled(step_a, image_a)
    steps = jnp.repeat(step_a, slab_image.shape[1] // step_a.shape[0])
    slab_b = (slab_residual - steps[None, :] * slab_image).astype(jnp.bfloat16)
    slab_b = slab_columns(slab_b.reshape(blocks_total, step_a.shape[0], -1))
    direction_b = finish(residual, slab_b, null_vectors, inverse_rows)
    image_b = apply_links(coarse_links, direction_b.astype(jnp.bfloat16))
    sums = total_sum(
        jnp.stack(
            [
                inner_rows(image_a, image_b),
                inner_rows(image_b, image_b),
                inner_rows(image_b, residual),
                inner_rows(image_a, residual),
            ]
        )
    )
    projection_sum, square_b, raw_correlation, shared_correlation = (
        sums[0], sums[1], sums[2], sums[3]
    )
    beta_coef = projection_sum / (norm_a + EPS)
    image_b = image_b - scaled(beta_coef, image_a)
    direction_b = direction_b - scaled(beta_coef, direction_a)
    norm_b = jnp.maximum(
        square_b - beta_coef * (2.0 * projection_sum - beta_coef * norm_a), 0.0
    )
    correlation_b = raw_correlation - beta_coef * shared_correlation
    step_b = correlation_b / (norm_b + EPS)
    solution = solution + scaled(step_b, direction_b)
    residual = residual - scaled(step_b, image_b)
    return (solution, residual)


def solution(mesh):
    in_specs = (
        P(None, "ta", "xyz", None, None, None, None),
        P("ta", "xyz", None, None, None, None, None, None),
        P("ta", "xyz", None, None, None, None, None),
        P("ta", "xyz", None),
    )
    out_specs = (
        P(None, "ta", "xyz", None, None, None, None),
        P(None, "ta", "xyz", None, None, None, None),
    )
    return jax.shard_map(shards, mesh=mesh, in_specs=in_specs, out_specs=out_specs, check_vma=False)
```

```python
import jax
import jax.numpy as jnp
from jax import lax
from jax.sharding import PartitionSpec as P

OMEGA = 0.4
EPS = 1e-06


def is_power_of_two(count):
    return count & (count - 1) == 0


def exchange(x, axis, bit):
    count = lax.axis_size(axis)
    return lax.ppermute(x, axis, [(i, i ^ bit) for i in range(count)])


def axis_sum(x, axis):
    count = lax.axis_size(axis)
    if not is_power_of_two(count):
        return lax.psum(x, axis)
    bit = 1
    while bit < count:
        x = x + exchange(x, axis, bit)
        bit *= 2
    return x


def total_sum(x):
    axes = ("ta", "xyz")
    count = lax.axis_size("ta") * lax.axis_size("xyz")
    flat = x.reshape(-1)
    copies = jnp.broadcast_to(flat[None, None], (count, 1) + flat.shape)
    return jnp.sum(lax.all_to_all(copies, axes, 0, 0)[:, 0], axis=0).reshape(x.shape)


def neighbour_source(device, stride, extent, step):
    coord = device // stride % extent
    return device + ((coord + step) % extent - coord) * stride


def both_sides(lowered, which, axis, stride, extent):
    length = lowered.shape[which]
    count = lax.axis_size(axis)
    first = lax.slice_in_dim(lowered, 0, 1, axis=which)
    last = lax.slice_in_dim(lowered, length - 1, length, axis=which)
    if extent == 1:
        from_upper, from_lower = first, last
    elif extent == 2:
        perm = [(neighbour_source(d, stride, extent, 1), d) for d in range(count)]
        if length == 1:
            from_upper = from_lower = lax.ppermute(first, axis, perm)
        else:
            pair = lax.ppermute(jnp.concatenate([first, last], which), axis, perm)
            from_upper = lax.slice_in_dim(pair, 0, 1, axis=which)
            from_lower = lax.slice_in_dim(pair, 1, 2, axis=which)
    else:
        up = [(neighbour_source(d, stride, extent, 1), d) for d in range(count)]
        down = [(neighbour_source(d, stride, extent, -1), d) for d in range(count)]
        from_upper = lax.ppermute(first, axis, up)
        from_lower = lax.ppermute(last, axis, down)
    upper = jnp.concatenate([lax.slice_in_dim(lowered, 1, length, axis=which), from_upper], which)
    lower = jnp.concatenate(
        [from_lower, lax.slice_in_dim(lowered, 0, length - 1, axis=which)], which
    )
    return (upper, lower)


def apply_links(coarse_links, lowered):
    blocks_total = lax.axis_size("xyz")
    across_x = 2 + 2 * min(blocks_total // 64, 1)
    across_z = blocks_total // (across_x * across_x)
    upper_x, lower_x = both_sides(lowered, 5, "xyz", 1, across_x)
    upper_y, lower_y = both_sides(lowered, 4, "xyz", across_x, across_x)
    upper_z, lower_z = both_sides(lowered, 3, "xyz", across_x * across_x, across_z)
    upper_t, lower_t = both_sides(lowered, 1, "ta", 1, lax.axis_size("ta"))
    stacked = jnp.stack(
        [lowered, upper_x, lower_x, upper_y, lower_y, upper_z, lower_z, upper_t, lower_t], 2
    )
    half_width = lowered.shape[-1] // 2
    real_part = stacked[..., :half_width]
    imag_part = stacked[..., half_width:]
    real_input = jnp.concatenate([real_part, -imag_part], -1)
    imag_input = jnp.concatenate([imag_part, real_part], -1)
    inputs = jnp.stack([real_input, imag_input], 0)
    result = jnp.einsum(
        "tbzyxdik,pntdbzyxk->pntbzyxi", coarse_links, inputs, preferred_element_type=jnp.float32
    )
    return jnp.concatenate([result[0], result[1]], -1)


def restrict_exact(null_vectors, field):
    return jnp.einsum(
        "tbzyxjk,ntbzyxk->nj",
        null_vectors.astype(jnp.float32),
        field,
        preferred_element_type=jnp.float32,
        precision=lax.Precision.HIGH,
    )


def slab_columns(parts):
    return jnp.transpose(parts, (1, 0, 2)).reshape(parts.shape[1], -1)


def finish(vector_in, slab, null_vectors, inverse_rows):
    correction = lax.dot_general(
        slab,
        inverse_rows,
        (((1,), (1,)), ((), ())),
        preferred_element_type=jnp.float32,
    ).astype(jnp.bfloat16)
    prolonged = jnp.einsum(
        "tbzyxjk,nj->ntbzyxk", null_vectors, correction, preferred_element_type=jnp.float32
    )
    return OMEGA * vector_in + prolonged


def inner_rows(left_vec, right_vec):
    return jnp.sum(left_vec * right_vec, axis=(1, 2, 3, 4, 5, 6))


def scaled(weights, vector_in):
    return weights[:, None, None, None, None, None, None] * vector_in


def shards(right_side, coarse_links, null_vectors, coarse_inverse):
    inverse_rows = coarse_inverse[0]
    slabs_total = lax.axis_size("ta")
    blocks_total = lax.axis_size("xyz")
    residual = right_side
    high = residual.astype(jnp.bfloat16)
    low = (residual - high.astype(jnp.float32)).astype(jnp.bfloat16)
    both = jnp.einsum(
        "tbzyxjk,sntbzyxk->snj",
        null_vectors,
        jnp.stack([high, low]),
        preferred_element_type=jnp.float32,
    )
    coarse = both[0].astype(jnp.bfloat16)
    width = coarse.shape[1]
    payload = jnp.concatenate([coarse.astype(jnp.float32), both[0] + both[1]], 1)
    parts = lax.all_to_all(
        jnp.broadcast_to(payload[None], (blocks_total,) + payload.shape), "xyz", 0, 0
    )
    slab_a = slab_columns(parts[:, :, :width]).astype(jnp.bfloat16)
    slab_residual = parts[:, :, width:].reshape(blocks_total, -1)
    direction_a = finish(residual, slab_a, null_vectors, inverse_rows)
    image_a = apply_links(coarse_links, direction_a.astype(jnp.bfloat16))
    image_coarse = restrict_exact(null_vectors, image_a)
    pair_local = jnp.stack([inner_rows(image_a, image_a), inner_rows(image_a, residual)], 1)
    if slabs_total * blocks_total <= 64:
        devices = slabs_total * blocks_total
        count, width = image_coarse.shape
        local = jnp.concatenate([pair_local.T.reshape(-1), image_coarse.reshape(-1)])
        gathered = lax.all_to_all(
            jnp.broadcast_to(local[None, None], (devices, 1) + local.shape),
            ("ta", "xyz"),
            0,
            0,
        )[:, 0]
        pair = jnp.sum(gathered[:, : 2 * count], axis=0).reshape(2, count).T
        image_slabs = gathered[:, 2 * count :].reshape(
            (slabs_total, blocks_total, count * width)
        )
        slab_image = lax.dynamic_index_in_dim(
            image_slabs, lax.axis_index("ta"), 0, keepdims=False
        )
    else:
        pair = total_sum(pair_local)
        slab_image = lax.all_to_all(
            jnp.broadcast_to(image_coarse[None], (blocks_total,) + image_coarse.shape),
            "xyz",
            0,
            0,
        ).reshape(blocks_total, -1)
    norm_a, correlation_a = pair[:, 0], pair[:, 1]
    step_a = correlation_a / (norm_a + EPS)
    solution = scaled(step_a, direction_a)
    residual = residual - scaled(step_a, image_a)
    steps = jnp.repeat(step_a, slab_image.shape[1] // step_a.shape[0])
    slab_b = (slab_residual - steps[None, :] * slab_image).astype(jnp.bfloat16)
    slab_b = slab_columns(slab_b.reshape(blocks_total, step_a.shape[0], -1))
    direction_b = finish(residual, slab_b, null_vectors, inverse_rows)
    image_b = apply_links(coarse_links, direction_b.astype(jnp.bfloat16))
    sums = total_sum(
        jnp.stack(
            [
                inner_rows(image_a, image_b),
                inner_rows(image_b, image_b),
                inner_rows(image_b, residual),
                inner_rows(image_a, residual),
            ]
        )
    )
    projection_sum, square_b, raw_correlation, shared_correlation = (
        sums[0], sums[1], sums[2], sums[3]
    )
    beta_coef = projection_sum / (norm_a + EPS)
    image_b = image_b - scaled(beta_coef, image_a)
    direction_b = direction_b - scaled(beta_coef, direction_a)
    norm_b = jnp.maximum(
        square_b - beta_coef * (2.0 * projection_sum - beta_coef * norm_a), 0.0
    )
    correlation_b = raw_correlation - beta_coef * shared_correlation
    step_b = correlation_b / (norm_b + EPS)
    solution = solution + scaled(step_b, direction_b)
    residual = residual - scaled(step_b, image_b)
    return (solution, residual)


def solution(mesh):
    in_specs = (
        P(None, "ta", "xyz", None, None, None, None),
        P("ta", "xyz", None, None, None, None, None, None),
        P("ta", "xyz", None, None, None, None, None),
        P("ta", "xyz", None),
    )
    out_specs = (
        P(None, "ta", "xyz", None, None, None, None),
        P(None, "ta", "xyz", None, None, None, None),
    )
    return jax.shard_map(shards, mesh=mesh, in_specs=in_specs, out_specs=out_specs, check_vma=False)
```

```python
import jax
import jax.numpy as jnp
from jax import lax
from jax.sharding import PartitionSpec as P

OMEGA = 0.4
EPS = 1e-06


def is_power_of_two(count):
    return count & (count - 1) == 0


def exchange(x, axis, bit):
    count = lax.axis_size(axis)
    return lax.ppermute(x, axis, [(i, i ^ bit) for i in range(count)])


def axis_sum(x, axis):
    count = lax.axis_size(axis)
    if not is_power_of_two(count):
        return lax.psum(x, axis)
    bit = 1
    while bit < count:
        x = x + exchange(x, axis, bit)
        bit *= 2
    return x


def total_sum(x):
    axes = ("ta", "xyz")
    count = lax.axis_size("ta") * lax.axis_size("xyz")
    flat = x.reshape(-1)
    copies = jnp.broadcast_to(flat[None, None], (count, 1) + flat.shape)
    return jnp.sum(lax.all_to_all(copies, axes, 0, 0)[:, 0], axis=0).reshape(x.shape)


def neighbour_source(device, stride, extent, step):
    coord = device // stride % extent
    return device + ((coord + step) % extent - coord) * stride


def both_sides(lowered, which, axis, stride, extent):
    length = lowered.shape[which]
    count = lax.axis_size(axis)
    first = lax.slice_in_dim(lowered, 0, 1, axis=which)
    last = lax.slice_in_dim(lowered, length - 1, length, axis=which)
    if extent == 1:
        from_upper, from_lower = first, last
    elif extent == 2:
        perm = [(neighbour_source(d, stride, extent, 1), d) for d in range(count)]
        if length == 1:
            from_upper = from_lower = lax.ppermute(first, axis, perm)
        else:
            pair = lax.ppermute(jnp.concatenate([first, last], which), axis, perm)
            from_upper = lax.slice_in_dim(pair, 0, 1, axis=which)
            from_lower = lax.slice_in_dim(pair, 1, 2, axis=which)
    else:
        up = [(neighbour_source(d, stride, extent, 1), d) for d in range(count)]
        down = [(neighbour_source(d, stride, extent, -1), d) for d in range(count)]
        from_upper = lax.ppermute(first, axis, up)
        from_lower = lax.ppermute(last, axis, down)
    upper = jnp.concatenate([lax.slice_in_dim(lowered, 1, length, axis=which), from_upper], which)
    lower = jnp.concatenate(
        [from_lower, lax.slice_in_dim(lowered, 0, length - 1, axis=which)], which
    )
    return (upper, lower)


def apply_links(links_pair, lowered):
    blocks_total = lax.axis_size("xyz")
    across_x = 2 + 2 * min(blocks_total // 64, 1)
    across_z = blocks_total // (across_x * across_x)
    upper_x, lower_x = both_sides(lowered, 5, "xyz", 1, across_x)
    upper_y, lower_y = both_sides(lowered, 4, "xyz", across_x, across_x)
    upper_z, lower_z = both_sides(lowered, 3, "xyz", across_x * across_x, across_z)
    upper_t, lower_t = both_sides(lowered, 1, "ta", 1, lax.axis_size("ta"))
    stacked = jnp.stack(
        [lowered, upper_x, lower_x, upper_y, lower_y, upper_z, lower_z, upper_t, lower_t], 2
    )
    real_links, imag_links = links_pair
    real = jnp.einsum(
        "tbzyxdik,ntdbzyxk->ntbzyxi", real_links, stacked, preferred_element_type=jnp.float32
    )
    imag = jnp.einsum(
        "tbzyxdik,ntdbzyxk->ntbzyxi", imag_links, stacked, preferred_element_type=jnp.float32
    )
    return jnp.concatenate([real, imag], -1)


def split_links(coarse_links):
    half_width = coarse_links.shape[-1] // 2
    real_part = coarse_links[..., :half_width]
    imag_part = coarse_links[..., half_width:]
    return (
        jnp.concatenate([real_part, -imag_part], -1),
        jnp.concatenate([imag_part, real_part], -1),
    )


def restrict_exact(null_vectors, field):
    return jnp.einsum(
        "tbzyxjk,ntbzyxk->nj",
        null_vectors.astype(jnp.float32),
        field,
        preferred_element_type=jnp.float32,
        precision=lax.Precision.HIGH,
    )


def slab_columns(parts):
    return jnp.transpose(parts, (1, 0, 2)).reshape(parts.shape[1], -1)


def finish(vector_in, slab, null_vectors, inverse_rows):
    correction = lax.dot_general(
        slab,
        inverse_rows,
        (((1,), (1,)), ((), ())),
        preferred_element_type=jnp.float32,
    ).astype(jnp.bfloat16)
    prolonged = jnp.einsum(
        "tbzyxjk,nj->ntbzyxk", null_vectors, correction, preferred_element_type=jnp.float32
    )
    return OMEGA * vector_in + prolonged


def inner_rows(left_vec, right_vec):
    return jnp.sum(left_vec * right_vec, axis=(1, 2, 3, 4, 5, 6))


def scaled(weights, vector_in):
    return weights[:, None, None, None, None, None, None] * vector_in


def shards(right_side, coarse_links, null_vectors, coarse_inverse):
    inverse_rows = coarse_inverse[0]
    links_pair = split_links(coarse_links)
    slabs_total = lax.axis_size("ta")
    blocks_total = lax.axis_size("xyz")
    residual = right_side
    coarse = jnp.einsum(
        "tbzyxjk,ntbzyxk->nj",
        null_vectors,
        residual.astype(jnp.bfloat16),
        preferred_element_type=jnp.float32,
    ).astype(jnp.bfloat16)
    width = coarse.shape[1]
    payload = jnp.concatenate(
        [coarse.astype(jnp.float32), restrict_exact(null_vectors, residual)], 1
    )
    parts = lax.all_to_all(
        jnp.broadcast_to(payload[None], (blocks_total,) + payload.shape), "xyz", 0, 0
    )
    slab_a = slab_columns(parts[:, :, :width]).astype(jnp.bfloat16)
    slab_residual = parts[:, :, width:].reshape(blocks_total, -1)
    direction_a = finish(residual, slab_a, null_vectors, inverse_rows)
    image_a = apply_links(links_pair, direction_a.astype(jnp.bfloat16))
    image_coarse = restrict_exact(null_vectors, image_a)
    pair_local = jnp.stack([inner_rows(image_a, image_a), inner_rows(image_a, residual)], 1)
    if slabs_total * blocks_total <= 64:
        devices = slabs_total * blocks_total
        count, width = image_coarse.shape
        local = jnp.concatenate([pair_local.T.reshape(-1), image_coarse.reshape(-1)])
        gathered = lax.all_to_all(
            jnp.broadcast_to(local[None, None], (devices, 1) + local.shape),
            ("ta", "xyz"),
            0,
            0,
        )[:, 0]
        pair = jnp.sum(gathered[:, : 2 * count], axis=0).reshape(2, count).T
        image_slabs = gathered[:, 2 * count :].reshape(
            (slabs_total, blocks_total, count * width)
        )
        slab_image = lax.dynamic_index_in_dim(
            image_slabs, lax.axis_index("ta"), 0, keepdims=False
        )
    else:
        pair = total_sum(pair_local)
        slab_image = lax.all_to_all(
            jnp.broadcast_to(image_coarse[None], (blocks_total,) + image_coarse.shape),
            "xyz",
            0,
            0,
        ).reshape(blocks_total, -1)
    norm_a, correlation_a = pair[:, 0], pair[:, 1]
    step_a = correlation_a / (norm_a + EPS)
    solution = scaled(step_a, direction_a)
    residual = residual - scaled(step_a, image_a)
    steps = jnp.repeat(step_a, slab_image.shape[1] // step_a.shape[0])
    slab_b = (slab_residual - steps[None, :] * slab_image).astype(jnp.bfloat16)
    slab_b = slab_columns(slab_b.reshape(blocks_total, step_a.shape[0], -1))
    direction_b = finish(residual, slab_b, null_vectors, inverse_rows)
    image_b = apply_links(links_pair, direction_b.astype(jnp.bfloat16))
    sums = total_sum(
        jnp.stack(
            [
                inner_rows(image_a, image_b),
                inner_rows(image_b, image_b),
                inner_rows(image_b, residual),
                inner_rows(image_a, residual),
            ]
        )
    )
    projection_sum, square_b, raw_correlation, shared_correlation = (
        sums[0], sums[1], sums[2], sums[3]
    )
    beta_coef = projection_sum / (norm_a + EPS)
    image_b = image_b - scaled(beta_coef, image_a)
    direction_b = direction_b - scaled(beta_coef, direction_a)
    norm_b = jnp.maximum(
        square_b - beta_coef * (2.0 * projection_sum - beta_coef * norm_a), 0.0
    )
    correlation_b = raw_correlation - beta_coef * shared_correlation
    step_b = correlation_b / (norm_b + EPS)
    solution = solution + scaled(step_b, direction_b)
    residual = residual - scaled(step_b, image_b)
    return (solution, residual)


def solution(mesh):
    in_specs = (
        P(None, "ta", "xyz", None, None, None, None),
        P("ta", "xyz", None, None, None, None, None, None),
        P("ta", "xyz", None, None, None, None, None),
        P("ta", "xyz", None),
    )
    out_specs = (
        P(None, "ta", "xyz", None, None, None, None),
        P(None, "ta", "xyz", None, None, None, None),
    )
    return jax.shard_map(shards, mesh=mesh, in_specs=in_specs, out_specs=out_specs, check_vma=False)
```

```python
import jax
import jax.numpy as jnp
from jax import lax
from jax.sharding import PartitionSpec as P

OMEGA = 0.4
EPS = 1e-06


def is_power_of_two(count):
    return count & (count - 1) == 0


def exchange(x, axis, bit):
    count = lax.axis_size(axis)
    return lax.ppermute(x, axis, [(i, i ^ bit) for i in range(count)])


def axis_sum(x, axis):
    count = lax.axis_size(axis)
    if not is_power_of_two(count):
        return lax.psum(x, axis)
    bit = 1
    while bit < count:
        x = x + exchange(x, axis, bit)
        bit *= 2
    return x


def total_sum(x):
    axes = ("ta", "xyz")
    count = lax.axis_size("ta") * lax.axis_size("xyz")
    flat = x.reshape(-1)
    copies = jnp.broadcast_to(flat[None, None], (count, 1) + flat.shape)
    return jnp.sum(lax.all_to_all(copies, axes, 0, 0)[:, 0], axis=0).reshape(x.shape)


def neighbour_source(device, stride, extent, step):
    coord = device // stride % extent
    return device + ((coord + step) % extent - coord) * stride


def both_sides(lowered, which, axis, stride, extent):
    length = lowered.shape[which]
    count = lax.axis_size(axis)
    first = lax.slice_in_dim(lowered, 0, 1, axis=which)
    last = lax.slice_in_dim(lowered, length - 1, length, axis=which)
    if extent == 1:
        from_upper, from_lower = first, last
    elif extent == 2:
        perm = [(neighbour_source(d, stride, extent, 1), d) for d in range(count)]
        if length == 1:
            from_upper = from_lower = lax.ppermute(first, axis, perm)
        else:
            pair = lax.ppermute(jnp.concatenate([first, last], which), axis, perm)
            from_upper = lax.slice_in_dim(pair, 0, 1, axis=which)
            from_lower = lax.slice_in_dim(pair, 1, 2, axis=which)
    else:
        up = [(neighbour_source(d, stride, extent, 1), d) for d in range(count)]
        down = [(neighbour_source(d, stride, extent, -1), d) for d in range(count)]
        from_upper = lax.ppermute(first, axis, up)
        from_lower = lax.ppermute(last, axis, down)
    upper = jnp.concatenate([lax.slice_in_dim(lowered, 1, length, axis=which), from_upper], which)
    lower = jnp.concatenate(
        [from_lower, lax.slice_in_dim(lowered, 0, length - 1, axis=which)], which
    )
    return (upper, lower)


def apply_links(coarse_links, lowered):
    blocks_total = lax.axis_size("xyz")
    across_x = 2 + 2 * min(blocks_total // 64, 1)
    across_z = blocks_total // (across_x * across_x)
    upper_x, lower_x = both_sides(lowered, 5, "xyz", 1, across_x)
    upper_y, lower_y = both_sides(lowered, 4, "xyz", across_x, across_x)
    upper_z, lower_z = both_sides(lowered, 3, "xyz", across_x * across_x, across_z)
    upper_t, lower_t = both_sides(lowered, 1, "ta", 1, lax.axis_size("ta"))
    stacked = jnp.stack(
        [lowered, upper_x, lower_x, upper_y, lower_y, upper_z, lower_z, upper_t, lower_t], 2
    )
    half_width = lowered.shape[-1] // 2
    real_part = stacked[..., :half_width]
    imag_part = stacked[..., half_width:]
    real_input = jnp.concatenate([real_part, -imag_part], -1)
    imag_input = jnp.concatenate([imag_part, real_part], -1)
    inputs = jnp.stack([real_input, imag_input], 0)
    result = jnp.einsum(
        "tbzyxdik,pntdbzyxk->pntbzyxi", coarse_links, inputs, preferred_element_type=jnp.float32
    )
    return jnp.concatenate([result[0], result[1]], -1)


def restrict_exact(null_vectors, field):
    return jnp.einsum(
        "tbzyxjk,ntbzyxk->nj",
        null_vectors,
        field.astype(jnp.bfloat16),
        preferred_element_type=jnp.float32,
    )


def slab_columns(parts):
    return jnp.transpose(parts, (1, 0, 2)).reshape(parts.shape[1], -1)


def finish(vector_in, slab, null_vectors, inverse_rows):
    correction = lax.dot_general(
        slab,
        inverse_rows,
        (((1,), (1,)), ((), ())),
        preferred_element_type=jnp.float32,
    ).astype(jnp.bfloat16)
    prolonged = jnp.einsum(
        "tbzyxjk,nj->ntbzyxk", null_vectors, correction, preferred_element_type=jnp.float32
    )
    return OMEGA * vector_in + prolonged


def inner_rows(left_vec, right_vec):
    return jnp.sum(left_vec * right_vec, axis=(1, 2, 3, 4, 5, 6))


def scaled(weights, vector_in):
    return weights[:, None, None, None, None, None, None] * vector_in


def shards(right_side, coarse_links, null_vectors, coarse_inverse):
    inverse_rows = coarse_inverse[0]
    slabs_total = lax.axis_size("ta")
    blocks_total = lax.axis_size("xyz")
    residual = right_side
    exact_residual = restrict_exact(null_vectors, residual)
    count, width = exact_residual.shape
    flat = exact_residual.reshape(-1)
    parts = lax.all_to_all(
        jnp.broadcast_to(flat[None, None], (blocks_total, 1) + flat.shape), "xyz", 0, 0
    )[:, 0]
    slab_residual = parts
    slab_a = slab_columns(parts.reshape(blocks_total, count, width)).astype(jnp.bfloat16)
    direction_a = finish(residual, slab_a, null_vectors, inverse_rows)
    image_a = apply_links(coarse_links, direction_a.astype(jnp.bfloat16))
    image_coarse = restrict_exact(null_vectors, image_a)
    pair_local = jnp.stack([inner_rows(image_a, image_a), inner_rows(image_a, residual)], 1)
    if slabs_total * blocks_total <= 64:
        devices = slabs_total * blocks_total
        count, width = image_coarse.shape
        local = jnp.concatenate([pair_local.T.reshape(-1), image_coarse.reshape(-1)])
        gathered = lax.all_to_all(
            jnp.broadcast_to(local[None, None], (devices, 1) + local.shape),
            ("ta", "xyz"),
            0,
            0,
        )[:, 0]
        pair = jnp.sum(gathered[:, : 2 * count], axis=0).reshape(2, count).T
        image_slabs = gathered[:, 2 * count :].reshape(
            (slabs_total, blocks_total, count * width)
        )
        slab_image = lax.dynamic_index_in_dim(
            image_slabs, lax.axis_index("ta"), 0, keepdims=False
        )
    else:
        pair = total_sum(pair_local)
        slab_image = lax.all_to_all(
            jnp.broadcast_to(image_coarse[None], (blocks_total,) + image_coarse.shape),
            "xyz",
            0,
            0,
        ).reshape(blocks_total, -1)
    norm_a, correlation_a = pair[:, 0], pair[:, 1]
    step_a = correlation_a / (norm_a + EPS)
    solution = scaled(step_a, direction_a)
    residual = residual - scaled(step_a, image_a)
    steps = jnp.repeat(step_a, slab_image.shape[1] // step_a.shape[0])
    slab_b = (slab_residual - steps[None, :] * slab_image).astype(jnp.bfloat16)
    slab_b = slab_columns(slab_b.reshape(blocks_total, step_a.shape[0], -1))
    direction_b = finish(residual, slab_b, null_vectors, inverse_rows)
    image_b = apply_links(coarse_links, direction_b.astype(jnp.bfloat16))
    sums = total_sum(
        jnp.stack(
            [
                inner_rows(image_a, image_b),
                inner_rows(image_b, image_b),
                inner_rows(image_b, residual),
                inner_rows(image_a, residual),
            ]
        )
    )
    projection_sum, square_b, raw_correlation, shared_correlation = (
        sums[0], sums[1], sums[2], sums[3]
    )
    beta_coef = projection_sum / (norm_a + EPS)
    image_b = image_b - scaled(beta_coef, image_a)
    direction_b = direction_b - scaled(beta_coef, direction_a)
    norm_b = jnp.maximum(
        square_b - beta_coef * (2.0 * projection_sum - beta_coef * norm_a), 0.0
    )
    correlation_b = raw_correlation - beta_coef * shared_correlation
    step_b = correlation_b / (norm_b + EPS)
    solution = solution + scaled(step_b, direction_b)
    residual = residual - scaled(step_b, image_b)
    return (solution, residual)


def solution(mesh):
    in_specs = (
        P(None, "ta", "xyz", None, None, None, None),
        P("ta", "xyz", None, None, None, None, None, None),
        P("ta", "xyz", None, None, None, None, None),
        P("ta", "xyz", None),
    )
    out_specs = (
        P(None, "ta", "xyz", None, None, None, None),
        P(None, "ta", "xyz", None, None, None, None),
    )
    return jax.shard_map(shards, mesh=mesh, in_specs=in_specs, out_specs=out_specs, check_vma=False)
```

```python
import jax
import jax.numpy as jnp
from jax import lax
from jax.sharding import PartitionSpec as P

OMEGA = 0.4
EPS = 1e-06


def is_power_of_two(count):
    return count & (count - 1) == 0


def exchange(x, axis, bit):
    count = lax.axis_size(axis)
    return lax.ppermute(x, axis, [(i, i ^ bit) for i in range(count)])


def axis_sum(x, axis):
    count = lax.axis_size(axis)
    if not is_power_of_two(count):
        return lax.psum(x, axis)
    bit = 1
    while bit < count:
        x = x + exchange(x, axis, bit)
        bit *= 2
    return x


def total_sum(x):
    axes = ("ta", "xyz")
    count = lax.axis_size("ta") * lax.axis_size("xyz")
    flat = x.reshape(-1)
    copies = jnp.broadcast_to(flat[None, None], (count, 1) + flat.shape)
    return jnp.sum(lax.all_to_all(copies, axes, 0, 0)[:, 0], axis=0).reshape(x.shape)


def neighbour_source(device, stride, extent, step):
    coord = device // stride % extent
    return device + ((coord + step) % extent - coord) * stride


def both_sides(lowered, which, axis, stride, extent):
    length = lowered.shape[which]
    count = lax.axis_size(axis)
    first = lax.slice_in_dim(lowered, 0, 1, axis=which)
    last = lax.slice_in_dim(lowered, length - 1, length, axis=which)
    if extent == 1:
        from_upper, from_lower = first, last
    elif extent == 2:
        perm = [(neighbour_source(d, stride, extent, 1), d) for d in range(count)]
        if length == 1:
            from_upper = from_lower = lax.ppermute(first, axis, perm)
        else:
            pair = lax.ppermute(jnp.concatenate([first, last], which), axis, perm)
            from_upper = lax.slice_in_dim(pair, 0, 1, axis=which)
            from_lower = lax.slice_in_dim(pair, 1, 2, axis=which)
    else:
        up = [(neighbour_source(d, stride, extent, 1), d) for d in range(count)]
        down = [(neighbour_source(d, stride, extent, -1), d) for d in range(count)]
        from_upper = lax.ppermute(first, axis, up)
        from_lower = lax.ppermute(last, axis, down)
    upper = jnp.concatenate([lax.slice_in_dim(lowered, 1, length, axis=which), from_upper], which)
    lower = jnp.concatenate(
        [from_lower, lax.slice_in_dim(lowered, 0, length - 1, axis=which)], which
    )
    return (upper, lower)


def apply_links(coarse_links, lowered):
    blocks_total = lax.axis_size("xyz")
    across_x = 2 + 2 * min(blocks_total // 64, 1)
    across_z = blocks_total // (across_x * across_x)
    upper_x, lower_x = both_sides(lowered, 5, "xyz", 1, across_x)
    upper_y, lower_y = both_sides(lowered, 4, "xyz", across_x, across_x)
    upper_z, lower_z = both_sides(lowered, 3, "xyz", across_x * across_x, across_z)
    upper_t, lower_t = both_sides(lowered, 1, "ta", 1, lax.axis_size("ta"))
    stacked = jnp.stack(
        [lowered, upper_x, lower_x, upper_y, lower_y, upper_z, lower_z, upper_t, lower_t], 2
    )
    half_width = lowered.shape[-1] // 2
    real_part = stacked[..., :half_width]
    imag_part = stacked[..., half_width:]
    real_input = jnp.concatenate([real_part, -imag_part], -1)
    imag_input = jnp.concatenate([imag_part, real_part], -1)
    inputs = jnp.stack([real_input, imag_input], 0)
    result = jnp.einsum(
        "tbzyxdik,pntdbzyxk->pntbzyxi", coarse_links, inputs, preferred_element_type=jnp.float32
    )
    return jnp.concatenate([result[0], result[1]], -1)


def restrict_exact(null_vectors, field):
    return jnp.einsum(
        "tbzyxjk,ntbzyxk->nj",
        null_vectors.astype(jnp.float32),
        field,
        preferred_element_type=jnp.float32,
        precision=lax.Precision.HIGH,
    )


def slab_columns(parts):
    return jnp.transpose(parts, (1, 0, 2)).reshape(parts.shape[1], -1)


def finish(vector_in, slab, null_vectors, inverse_rows):
    correction = lax.dot_general(
        slab,
        inverse_rows,
        (((1,), (1,)), ((), ())),
        preferred_element_type=jnp.float32,
    ).astype(jnp.bfloat16)
    prolonged = jnp.einsum(
        "tbzyxjk,nj->ntbzyxk", null_vectors, correction, preferred_element_type=jnp.float32
    )
    return OMEGA * vector_in + prolonged


def inner_rows(left_vec, right_vec):
    return jnp.sum(left_vec * right_vec, axis=(1, 2, 3, 4, 5, 6))


def scaled(weights, vector_in):
    return weights[:, None, None, None, None, None, None] * vector_in


def shards(right_side, coarse_links, null_vectors, coarse_inverse):
    inverse_rows = coarse_inverse[0]
    slabs_total = lax.axis_size("ta")
    blocks_total = lax.axis_size("xyz")
    residual = right_side
    coarse = jnp.einsum(
        "tbzyxjk,ntbzyxk->nj",
        null_vectors,
        residual.astype(jnp.bfloat16),
        preferred_element_type=jnp.float32,
    ).astype(jnp.bfloat16)
    width = coarse.shape[1]
    payload = jnp.concatenate(
        [coarse.astype(jnp.float32), restrict_exact(null_vectors, residual)], 1
    )
    parts = lax.all_to_all(
        jnp.broadcast_to(payload[None], (blocks_total,) + payload.shape), "xyz", 0, 0
    )
    slab_a = slab_columns(parts[:, :, :width]).astype(jnp.bfloat16)
    slab_residual = parts[:, :, width:].reshape(blocks_total, -1)
    direction_a = finish(residual, slab_a, null_vectors, inverse_rows)
    image_a = apply_links(coarse_links, direction_a.astype(jnp.bfloat16))
    image_coarse = restrict_exact(null_vectors, image_a)
    pair_local = jnp.stack([inner_rows(image_a, image_a), inner_rows(image_a, residual)], 1)
    if slabs_total * blocks_total <= 64:
        devices = slabs_total * blocks_total
        count, width = image_coarse.shape
        pair_flat = pair_local.T.reshape(-1)
        high = pair_flat.astype(jnp.bfloat16)
        low = (pair_flat - high.astype(jnp.float32)).astype(jnp.bfloat16)
        local = jnp.concatenate([high, low, image_coarse.reshape(-1).astype(jnp.bfloat16)])
        gathered = lax.all_to_all(
            jnp.broadcast_to(local[None, None], (devices, 1) + local.shape),
            ("ta", "xyz"),
            0,
            0,
        )[:, 0]
        size = pair_flat.shape[0]
        pair_parts = gathered[:, :size].astype(jnp.float32) + gathered[
            :, size : 2 * size
        ].astype(jnp.float32)
        pair = jnp.sum(pair_parts, axis=0).reshape(2, count).T
        image_slabs = gathered[:, 2 * size :].astype(jnp.float32).reshape(
            (slabs_total, blocks_total, count * width)
        )
        slab_image = lax.dynamic_index_in_dim(
            image_slabs, lax.axis_index("ta"), 0, keepdims=False
        )
    else:
        pair = total_sum(pair_local)
        slab_image = lax.all_to_all(
            jnp.broadcast_to(image_coarse[None], (blocks_total,) + image_coarse.shape),
            "xyz",
            0,
            0,
        ).reshape(blocks_total, -1)
    norm_a, correlation_a = pair[:, 0], pair[:, 1]
    step_a = correlation_a / (norm_a + EPS)
    solution = scaled(step_a, direction_a)
    residual = residual - scaled(step_a, image_a)
    steps = jnp.repeat(step_a, slab_image.shape[1] // step_a.shape[0])
    slab_b = (slab_residual - steps[None, :] * slab_image).astype(jnp.bfloat16)
    slab_b = slab_columns(slab_b.reshape(blocks_total, step_a.shape[0], -1))
    direction_b = finish(residual, slab_b, null_vectors, inverse_rows)
    image_b = apply_links(coarse_links, direction_b.astype(jnp.bfloat16))
    sums = total_sum(
        jnp.stack(
            [
                inner_rows(image_a, image_b),
                inner_rows(image_b, image_b),
                inner_rows(image_b, residual),
                inner_rows(image_a, residual),
            ]
        )
    )
    projection_sum, square_b, raw_correlation, shared_correlation = (
        sums[0], sums[1], sums[2], sums[3]
    )
    beta_coef = projection_sum / (norm_a + EPS)
    image_b = image_b - scaled(beta_coef, image_a)
    direction_b = direction_b - scaled(beta_coef, direction_a)
    norm_b = jnp.maximum(
        square_b - beta_coef * (2.0 * projection_sum - beta_coef * norm_a), 0.0
    )
    correlation_b = raw_correlation - beta_coef * shared_correlation
    step_b = correlation_b / (norm_b + EPS)
    solution = solution + scaled(step_b, direction_b)
    residual = residual - scaled(step_b, image_b)
    return (solution, residual)


def solution(mesh):
    in_specs = (
        P(None, "ta", "xyz", None, None, None, None),
        P("ta", "xyz", None, None, None, None, None, None),
        P("ta", "xyz", None, None, None, None, None),
        P("ta", "xyz", None),
    )
    out_specs = (
        P(None, "ta", "xyz", None, None, None, None),
        P(None, "ta", "xyz", None, None, None, None),
    )
    return jax.shard_map(shards, mesh=mesh, in_specs=in_specs, out_specs=out_specs, check_vma=False)
```

```python
import jax
import jax.numpy as jnp
from jax import lax
from jax.sharding import PartitionSpec as P

OMEGA = 0.4
EPS = 1e-06


def is_power_of_two(count):
    return count & (count - 1) == 0


def exchange(x, axis, bit):
    count = lax.axis_size(axis)
    return lax.ppermute(x, axis, [(i, i ^ bit) for i in range(count)])


def axis_sum(x, axis):
    count = lax.axis_size(axis)
    if not is_power_of_two(count):
        return lax.psum(x, axis)
    bit = 1
    while bit < count:
        x = x + exchange(x, axis, bit)
        bit *= 2
    return x


def total_sum(x):
    axes = ("ta", "xyz")
    count = lax.axis_size("ta") * lax.axis_size("xyz")
    flat = x.reshape(-1)
    copies = jnp.broadcast_to(flat[None, None], (count, 1) + flat.shape)
    return jnp.sum(lax.all_to_all(copies, axes, 0, 0)[:, 0], axis=0).reshape(x.shape)


def neighbour_source(device, stride, extent, step):
    coord = device // stride % extent
    return device + ((coord + step) % extent - coord) * stride


def both_sides(lowered, which, axis, stride, extent):
    length = lowered.shape[which]
    count = lax.axis_size(axis)
    first = lax.slice_in_dim(lowered, 0, 1, axis=which)
    last = lax.slice_in_dim(lowered, length - 1, length, axis=which)
    if extent == 1:
        from_upper, from_lower = first, last
    elif extent == 2:
        perm = [(neighbour_source(d, stride, extent, 1), d) for d in range(count)]
        if length == 1:
            from_upper = from_lower = lax.ppermute(first, axis, perm)
        else:
            pair = lax.ppermute(jnp.concatenate([first, last], which), axis, perm)
            from_upper = lax.slice_in_dim(pair, 0, 1, axis=which)
            from_lower = lax.slice_in_dim(pair, 1, 2, axis=which)
    else:
        up = [(neighbour_source(d, stride, extent, 1), d) for d in range(count)]
        down = [(neighbour_source(d, stride, extent, -1), d) for d in range(count)]
        from_upper = lax.ppermute(first, axis, up)
        from_lower = lax.ppermute(last, axis, down)
    upper = jnp.concatenate([lax.slice_in_dim(lowered, 1, length, axis=which), from_upper], which)
    lower = jnp.concatenate(
        [from_lower, lax.slice_in_dim(lowered, 0, length - 1, axis=which)], which
    )
    return (upper, lower)


def apply_links(coarse_links, lowered):
    blocks_total = lax.axis_size("xyz")
    across_x = 2 + 2 * min(blocks_total // 64, 1)
    across_z = blocks_total // (across_x * across_x)
    upper_x, lower_x = both_sides(lowered, 5, "xyz", 1, across_x)
    upper_y, lower_y = both_sides(lowered, 4, "xyz", across_x, across_x)
    upper_z, lower_z = both_sides(lowered, 3, "xyz", across_x * across_x, across_z)
    upper_t, lower_t = both_sides(lowered, 1, "ta", 1, lax.axis_size("ta"))
    stacked = jnp.stack(
        [lowered, upper_x, lower_x, upper_y, lower_y, upper_z, lower_z, upper_t, lower_t], 2
    )
    half_width = lowered.shape[-1] // 2
    lanes = lax.broadcasted_iota(jnp.int32, (lowered.shape[-1],), 0)
    signs = jnp.where(lanes < half_width, 1.0, -1.0).astype(stacked.dtype)
    inputs = jnp.stack([stacked * signs, jnp.roll(stacked, half_width, axis=-1)], 0)
    result = jnp.einsum(
        "tbzyxdik,pntdbzyxk->pntbzyxi", coarse_links, inputs, preferred_element_type=jnp.float32
    )
    return jnp.concatenate([result[0], result[1]], -1)


def restrict_exact(null_vectors, field):
    return jnp.einsum(
        "tbzyxjk,ntbzyxk->nj",
        null_vectors.astype(jnp.float32),
        field,
        preferred_element_type=jnp.float32,
        precision=lax.Precision.HIGH,
    )


def slab_columns(parts):
    return jnp.transpose(parts, (1, 0, 2)).reshape(parts.shape[1], -1)


def finish(vector_in, slab, null_vectors, inverse_rows):
    correction = lax.dot_general(
        slab,
        inverse_rows,
        (((1,), (1,)), ((), ())),
        preferred_element_type=jnp.float32,
    ).astype(jnp.bfloat16)
    prolonged = jnp.einsum(
        "tbzyxjk,nj->ntbzyxk", null_vectors, correction, preferred_element_type=jnp.float32
    )
    return OMEGA * vector_in + prolonged


def inner_rows(left_vec, right_vec):
    return jnp.sum(left_vec * right_vec, axis=(1, 2, 3, 4, 5, 6))


def scaled(weights, vector_in):
    return weights[:, None, None, None, None, None, None] * vector_in


def shards(right_side, coarse_links, null_vectors, coarse_inverse):
    inverse_rows = coarse_inverse[0]
    slabs_total = lax.axis_size("ta")
    blocks_total = lax.axis_size("xyz")
    residual = right_side
    coarse = jnp.einsum(
        "tbzyxjk,ntbzyxk->nj",
        null_vectors,
        residual.astype(jnp.bfloat16),
        preferred_element_type=jnp.float32,
    ).astype(jnp.bfloat16)
    width = coarse.shape[1]
    payload = jnp.concatenate(
        [coarse.astype(jnp.float32), restrict_exact(null_vectors, residual)], 1
    )
    parts = lax.all_to_all(
        jnp.broadcast_to(payload[None], (blocks_total,) + payload.shape), "xyz", 0, 0
    )
    slab_a = slab_columns(parts[:, :, :width]).astype(jnp.bfloat16)
    slab_residual = parts[:, :, width:].reshape(blocks_total, -1)
    direction_a = finish(residual, slab_a, null_vectors, inverse_rows)
    image_a = apply_links(coarse_links, direction_a.astype(jnp.bfloat16))
    image_coarse = restrict_exact(null_vectors, image_a)
    pair_local = jnp.stack([inner_rows(image_a, image_a), inner_rows(image_a, residual)], 1)
    if slabs_total * blocks_total <= 64:
        devices = slabs_total * blocks_total
        count, width = image_coarse.shape
        local = jnp.concatenate([pair_local.T.reshape(-1), image_coarse.reshape(-1)])
        gathered = lax.all_to_all(
            jnp.broadcast_to(local[None, None], (devices, 1) + local.shape),
            ("ta", "xyz"),
            0,
            0,
        )[:, 0]
        pair = jnp.sum(gathered[:, : 2 * count], axis=0).reshape(2, count).T
        image_slabs = gathered[:, 2 * count :].reshape(
            (slabs_total, blocks_total, count * width)
        )
        slab_image = lax.dynamic_index_in_dim(
            image_slabs, lax.axis_index("ta"), 0, keepdims=False
        )
    else:
        pair = total_sum(pair_local)
        slab_image = lax.all_to_all(
            jnp.broadcast_to(image_coarse[None], (blocks_total,) + image_coarse.shape),
            "xyz",
            0,
            0,
        ).reshape(blocks_total, -1)
    norm_a, correlation_a = pair[:, 0], pair[:, 1]
    step_a = correlation_a / (norm_a + EPS)
    solution = scaled(step_a, direction_a)
    residual = residual - scaled(step_a, image_a)
    steps = jnp.repeat(step_a, slab_image.shape[1] // step_a.shape[0])
    slab_b = (slab_residual - steps[None, :] * slab_image).astype(jnp.bfloat16)
    slab_b = slab_columns(slab_b.reshape(blocks_total, step_a.shape[0], -1))
    direction_b = finish(residual, slab_b, null_vectors, inverse_rows)
    image_b = apply_links(coarse_links, direction_b.astype(jnp.bfloat16))
    sums = total_sum(
        jnp.stack(
            [
                inner_rows(image_a, image_b),
                inner_rows(image_b, image_b),
                inner_rows(image_b, residual),
                inner_rows(image_a, residual),
            ]
        )
    )
    projection_sum, square_b, raw_correlation, shared_correlation = (
        sums[0], sums[1], sums[2], sums[3]
    )
    beta_coef = projection_sum / (norm_a + EPS)
    image_b = image_b - scaled(beta_coef, image_a)
    direction_b = direction_b - scaled(beta_coef, direction_a)
    norm_b = jnp.maximum(
        square_b - beta_coef * (2.0 * projection_sum - beta_coef * norm_a), 0.0
    )
    correlation_b = raw_correlation - beta_coef * shared_correlation
    step_b = correlation_b / (norm_b + EPS)
    solution = solution + scaled(step_b, direction_b)
    residual = residual - scaled(step_b, image_b)
    return (solution, residual)


def solution(mesh):
    in_specs = (
        P(None, "ta", "xyz", None, None, None, None),
        P("ta", "xyz", None, None, None, None, None, None),
        P("ta", "xyz", None, None, None, None, None),
        P("ta", "xyz", None),
    )
    out_specs = (
        P(None, "ta", "xyz", None, None, None, None),
        P(None, "ta", "xyz", None, None, None, None),
    )
    return jax.shard_map(shards, mesh=mesh, in_specs=in_specs, out_specs=out_specs, check_vma=False)
```

```python
import jax
import jax.numpy as jnp
from jax import lax
from jax.experimental.layout import Layout, with_layout_constraint
from jax.sharding import PartitionSpec as P

OMEGA = 0.4
EPS = 1e-06


def is_power_of_two(count):
    return count & (count - 1) == 0


def exchange(x, axis, bit):
    count = lax.axis_size(axis)
    return lax.ppermute(x, axis, [(i, i ^ bit) for i in range(count)])


def axis_sum(x, axis):
    count = lax.axis_size(axis)
    if not is_power_of_two(count):
        return lax.psum(x, axis)
    bit = 1
    while bit < count:
        x = x + exchange(x, axis, bit)
        bit *= 2
    return x


def total_sum(x):
    axes = ("ta", "xyz")
    count = lax.axis_size("ta") * lax.axis_size("xyz")
    flat = x.reshape(-1)
    copies = jnp.broadcast_to(flat[None, None], (count, 1) + flat.shape)
    return jnp.sum(lax.all_to_all(copies, axes, 0, 0)[:, 0], axis=0).reshape(x.shape)


def neighbour_source(device, stride, extent, step):
    coord = device // stride % extent
    return device + ((coord + step) % extent - coord) * stride


def both_sides(lowered, which, axis, stride, extent):
    length = lowered.shape[which]
    count = lax.axis_size(axis)
    first = lax.slice_in_dim(lowered, 0, 1, axis=which)
    last = lax.slice_in_dim(lowered, length - 1, length, axis=which)
    if extent == 1:
        from_upper, from_lower = first, last
    elif extent == 2:
        perm = [(neighbour_source(d, stride, extent, 1), d) for d in range(count)]
        if length == 1:
            from_upper = from_lower = lax.ppermute(first, axis, perm)
        else:
            pair = lax.ppermute(jnp.concatenate([first, last], which), axis, perm)
            from_upper = lax.slice_in_dim(pair, 0, 1, axis=which)
            from_lower = lax.slice_in_dim(pair, 1, 2, axis=which)
    else:
        up = [(neighbour_source(d, stride, extent, 1), d) for d in range(count)]
        down = [(neighbour_source(d, stride, extent, -1), d) for d in range(count)]
        from_upper = lax.ppermute(first, axis, up)
        from_lower = lax.ppermute(last, axis, down)
    upper = jnp.concatenate([lax.slice_in_dim(lowered, 1, length, axis=which), from_upper], which)
    lower = jnp.concatenate(
        [from_lower, lax.slice_in_dim(lowered, 0, length - 1, axis=which)], which
    )
    return (upper, lower)


def apply_links(coarse_links, lowered):
    blocks_total = lax.axis_size("xyz")
    across_x = 2 + 2 * min(blocks_total // 64, 1)
    across_z = blocks_total // (across_x * across_x)
    upper_x, lower_x = both_sides(lowered, 5, "xyz", 1, across_x)
    upper_y, lower_y = both_sides(lowered, 4, "xyz", across_x, across_x)
    upper_z, lower_z = both_sides(lowered, 3, "xyz", across_x * across_x, across_z)
    upper_t, lower_t = both_sides(lowered, 1, "ta", 1, lax.axis_size("ta"))
    stacked = jnp.stack(
        [lowered, upper_x, lower_x, upper_y, lower_y, upper_z, lower_z, upper_t, lower_t], 2
    )
    half_width = lowered.shape[-1] // 2
    real_part = stacked[..., :half_width]
    imag_part = stacked[..., half_width:]
    real_input = jnp.concatenate([real_part, -imag_part], -1)
    imag_input = jnp.concatenate([imag_part, real_part], -1)
    inputs = jnp.stack([real_input, imag_input], 0)
    result = jnp.einsum(
        "tbzyxdik,pntdbzyxk->pntbzyxi", coarse_links, inputs, preferred_element_type=jnp.float32
    )
    return jnp.concatenate([result[0], result[1]], -1)


def restrict_exact(null_vectors, field):
    return jnp.einsum(
        "tbzyxjk,ntbzyxk->nj",
        null_vectors.astype(jnp.float32),
        field,
        preferred_element_type=jnp.float32,
        precision=lax.Precision.HIGH,
    )


def slab_columns(parts):
    return jnp.transpose(parts, (1, 0, 2)).reshape(parts.shape[1], -1)


def finish(vector_in, slab, null_vectors, inverse_rows):
    correction = lax.dot_general(
        slab,
        inverse_rows,
        (((1,), (1,)), ((), ())),
        preferred_element_type=jnp.float32,
    ).astype(jnp.bfloat16)
    prolonged = jnp.einsum(
        "tbzyxjk,nj->ntbzyxk", null_vectors, correction, preferred_element_type=jnp.float32
    )
    return OMEGA * vector_in + prolonged


def inner_rows(left_vec, right_vec):
    return jnp.sum(left_vec * right_vec, axis=(1, 2, 3, 4, 5, 6))


def scaled(weights, vector_in):
    return weights[:, None, None, None, None, None, None] * vector_in


def shards(right_side, coarse_links, null_vectors, coarse_inverse):
    inverse_rows = coarse_inverse[0]
    slabs_total = lax.axis_size("ta")
    blocks_total = lax.axis_size("xyz")
    residual = right_side
    coarse = jnp.einsum(
        "tbzyxjk,ntbzyxk->nj",
        null_vectors,
        residual.astype(jnp.bfloat16),
        preferred_element_type=jnp.float32,
    ).astype(jnp.bfloat16)
    width = coarse.shape[1]
    payload = jnp.concatenate(
        [coarse.astype(jnp.float32), restrict_exact(null_vectors, residual)], 1
    )
    parts = lax.all_to_all(
        jnp.broadcast_to(payload[None], (blocks_total,) + payload.shape), "xyz", 0, 0
    )
    slab_a = slab_columns(parts[:, :, :width]).astype(jnp.bfloat16)
    slab_residual = parts[:, :, width:].reshape(blocks_total, -1)
    direction_a = finish(residual, slab_a, null_vectors, inverse_rows)
    image_a = apply_links(coarse_links, direction_a.astype(jnp.bfloat16))
    image_coarse = restrict_exact(null_vectors, image_a)
    pair_local = jnp.stack([inner_rows(image_a, image_a), inner_rows(image_a, residual)], 1)
    if slabs_total * blocks_total <= 64:
        devices = slabs_total * blocks_total
        count, width = image_coarse.shape
        local = jnp.concatenate([pair_local.T.reshape(-1), image_coarse.reshape(-1)])
        gathered = lax.all_to_all(
            jnp.broadcast_to(local[None, None], (devices, 1) + local.shape),
            ("ta", "xyz"),
            0,
            0,
        )[:, 0]
        pair = jnp.sum(gathered[:, : 2 * count], axis=0).reshape(2, count).T
        image_slabs = gathered[:, 2 * count :].reshape(
            (slabs_total, blocks_total, count * width)
        )
        slab_image = lax.dynamic_index_in_dim(
            image_slabs, lax.axis_index("ta"), 0, keepdims=False
        )
    else:
        pair = total_sum(pair_local)
        slab_image = lax.all_to_all(
            jnp.broadcast_to(image_coarse[None], (blocks_total,) + image_coarse.shape),
            "xyz",
            0,
            0,
        ).reshape(blocks_total, -1)
    norm_a, correlation_a = pair[:, 0], pair[:, 1]
    step_a = correlation_a / (norm_a + EPS)
    solution = scaled(step_a, direction_a)
    residual = residual - scaled(step_a, image_a)
    steps = jnp.repeat(step_a, slab_image.shape[1] // step_a.shape[0])
    slab_b = (slab_residual - steps[None, :] * slab_image).astype(jnp.bfloat16)
    slab_b = slab_columns(slab_b.reshape(blocks_total, step_a.shape[0], -1))
    direction_b = finish(residual, slab_b, null_vectors, inverse_rows)
    image_b = apply_links(coarse_links, direction_b.astype(jnp.bfloat16))
    sums = total_sum(
        jnp.stack(
            [
                inner_rows(image_a, image_b),
                inner_rows(image_b, image_b),
                inner_rows(image_b, residual),
                inner_rows(image_a, residual),
            ]
        )
    )
    projection_sum, square_b, raw_correlation, shared_correlation = (
        sums[0], sums[1], sums[2], sums[3]
    )
    beta_coef = projection_sum / (norm_a + EPS)
    image_b = image_b - scaled(beta_coef, image_a)
    direction_b = direction_b - scaled(beta_coef, direction_a)
    norm_b = jnp.maximum(
        square_b - beta_coef * (2.0 * projection_sum - beta_coef * norm_a), 0.0
    )
    correlation_b = raw_correlation - beta_coef * shared_correlation
    step_b = correlation_b / (norm_b + EPS)
    solution = solution + scaled(step_b, direction_b)
    residual = residual - scaled(step_b, image_b)
    order = Layout(major_to_minor=tuple(range(solution.ndim)))
    return (with_layout_constraint(solution, order), with_layout_constraint(residual, order))


def solution(mesh):
    in_specs = (
        P(None, "ta", "xyz", None, None, None, None),
        P("ta", "xyz", None, None, None, None, None, None),
        P("ta", "xyz", None, None, None, None, None),
        P("ta", "xyz", None),
    )
    out_specs = (
        P(None, "ta", "xyz", None, None, None, None),
        P(None, "ta", "xyz", None, None, None, None),
    )
    return jax.shard_map(shards, mesh=mesh, in_specs=in_specs, out_specs=out_specs, check_vma=False)
```
